128 devices in a mesh: sub: 128 (over z, y, x, core).
Axes of the slice: x: 4, y: 4, z: 4, core: 2. Of those that a mesh axis runs over, the one named last changes fastest.
Arguments:
- pool_inputs: bfloat16 [65536, 4096], P('sub'), may hold values from -6 to 6
- pool_targets: bfloat16 [65536, 4096], P('sub'), may hold values from -6 to 6
- row_picks: int32 [8, 32768], P(None, 'sub'), may hold values from 0 to 511
- weight_in: float32 [4096, 32768], P(None, 'sub'), may hold values from -6 to 6
- weight_out: float32 [4096, 32768], P(None, 'sub'), may hold values from -6 to 6
- eval_inputs: bfloat16 [256, 4096], P('sub'), may hold values from -6 to 6
- handover: int32 [4096], replicated, may hold values from 0 to 4095, as said below
Outputs:
- trained_in: float32 [4096, 32768], P(None, 'sub')
- trained_out: float32 [4096, 32768], P(None, 'sub')
- prediction: float32 [256, 4096], P('sub')
The draws below stay inside these ranges and needn't reach their ends.
Inputs may be any that keep to these rules, and one draw needn't show every extreme that they name: `row_picks`: indices into the subnet's own 512 resident rows. handover[g] is the new position of neuron group g (neurons 8 g to 8 g + 7); every position is taken once, and no two groups of one subnet move to the same subnet.
All inputs are finite; a program needn't handle non-finite values.
Results may differ from the reference program's by a relative error of at most 0.0065.
Values may be sent and summed in bfloat16 or wider, within the bound.
No kernel may reach another device: no remote copies, remote signals or barrier semaphores. Data moves between devices by JAX's collectives and lax.ppermute only.
A program may use at most 192 MiB of HBM per device.

```python
import math
import jax
import jax.numpy as jnp
from jax import lax

D = 4096
HID_DEV = 256
GROUP = 8
STEPS = 4
BATCH = 256
POOL = 512
FF = 32768
GROUPS = 4096
POOLS = 65536
BATCHES = 32768
EVALS = 256


def unit_field(key, rows, columns):
    key_value = jax.random.fold_in(key, 0)
    return jax.random.truncated_normal(key_value, -6.0, 6.0, (rows, columns), jnp.float32)


def draw_pool_inputs(key, part):
    return unit_field(jax.random.fold_in(key, 11), POOLS, D).astype(jnp.bfloat16)


def draw_pool_targets(key, part):
    return unit_field(jax.random.fold_in(key, 12), POOLS, D).astype(jnp.bfloat16)


def draw_eval_inputs(key, part):
    return unit_field(jax.random.fold_in(key, 13), EVALS, D).astype(jnp.bfloat16)


def draw_weight_in(key, part):
    return unit_field(jax.random.fold_in(key, 14), D, FF).astype(jnp.float32)


def draw_weight_out(key, part):
    return unit_field(jax.random.fold_in(key, 15), D, FF).astype(jnp.float32)


def draw_handover(key, part):
    group_count = HID_DEV // GROUP
    owners = GROUPS // group_count
    key_relabel, key_shift, key_offset, key_source, key_slot = jax.random.split(key, 5)
    relabel = jax.random.permutation(key_relabel, owners).astype(jnp.int32)
    shifted = jax.random.permutation(key_shift, owners).astype(jnp.int32)
    offset_pick = jax.random.permutation(key_offset, owners).astype(jnp.int32)[:group_count]
    lane_index = jax.vmap(lambda one_key: jax.random.permutation(one_key, group_count))(jax.random.split(key_source, owners)).astype(jnp.int32)
    slot_order = jax.vmap(lambda one_key: jax.random.permutation(one_key, group_count))(jax.random.split(key_slot, owners)).astype(jnp.int32)
    destination = relabel[(shifted[:, None] + offset_pick[lane_index]) % owners]
    slot_index = slot_order[destination, lane_index]
    return (destination * group_count + slot_index).reshape(-1).astype(jnp.int32)


def plant(drawn, own_key, least, largest):
    place = [jax.random.randint(jax.random.fold_in(own_key, axis), (), 0, length) for axis, length in enumerate(drawn.shape)]
    main_axis = drawn.shape.index(max(drawn.shape))
    beside = place[:main_axis] + [(place[main_axis] + 1) % drawn.shape[main_axis]] + place[main_axis + 1:]
    return drawn.at[tuple(place)].set(least).at[tuple(beside)].set(largest)


def setup_inputs(seed: int = 0) -> dict:
    key_of = jax.random.split(jax.random.key(seed), 8)
    pool_inputs = draw_pool_inputs(jax.random.fold_in(key_of[7], 71), 0)
    pool_targets = draw_pool_targets(jax.random.fold_in(key_of[7], 71), 0)
    row_picks = plant(jax.random.randint(key_of[2], (2 * STEPS, BATCHES), 0, POOL), jax.random.fold_in(key_of[2], 1), 0, POOL - 1).astype(jnp.int32)
    weight_in = draw_weight_in(jax.random.fold_in(key_of[7], 71), 0)
    weight_out = draw_weight_out(jax.random.fold_in(key_of[7], 71), 0)
    eval_inputs = draw_eval_inputs(jax.random.fold_in(key_of[7], 71), 0)
    handover = draw_handover(jax.random.fold_in(key_of[7], 71), 0)
    return {"pool_inputs": pool_inputs, "pool_targets": pool_targets, "row_picks": row_picks, "weight_in": weight_in, "weight_out": weight_out, "eval_inputs": eval_inputs, "handover": handover}


tanh_coef = 0.7978845608028654
cubic_coef = 0.044715
step_rate = 0.5

def gelu_value(inputs):
    inner_term = tanh_coef * (inputs + cubic_coef * inputs * inputs * inputs)
    return 0.5 * inputs * (1.0 + jnp.tanh(inner_term))

def gelu_parts(inputs):
    tanh_part = jnp.tanh(tanh_coef * (inputs + cubic_coef * inputs * inputs * inputs))
    values = 0.5 * inputs * (1.0 + tanh_part)
    slopes = 0.5 * (1.0 + tanh_part) + 0.5 * inputs * (1.0 - tanh_part * tanh_part) * tanh_coef * (1.0 + 3.0 * cubic_coef * inputs * inputs)
    return (values, slopes)

def train_step(layer_in, layer_out, batch_rows, batch_goals, scale_in, scale_out):
    in_half = layer_in.astype(jnp.bfloat16)
    out_half = layer_out.astype(jnp.bfloat16)
    before = jnp.dot(batch_rows, in_half, preferred_element_type=jnp.float32) * scale_in
    values, slopes = gelu_parts(before)
    activity = values.astype(jnp.bfloat16)
    branch = jnp.dot(activity, out_half.T, preferred_element_type=jnp.float32) * scale_out
    errors = (branch - batch_goals.astype(jnp.float32)).astype(jnp.bfloat16)
    grad_out = jnp.dot(errors.T, activity, preferred_element_type=jnp.float32) * scale_out
    backward = (jnp.dot(errors, out_half, preferred_element_type=jnp.float32) * scale_out * slopes).astype(jnp.bfloat16)
    grad_in = jnp.dot(batch_rows.T, backward, preferred_element_type=jnp.float32) * scale_in
    return (layer_in - step_rate * grad_in, layer_out - step_rate * grad_out)

def run_round(weight_in, weight_out, pool_inputs, pool_targets, row_picks, first_turn):
    owners = FF // HID_DEV
    scale_in = 1.0 / math.sqrt(D)
    scale_out = 1.0 / math.sqrt(FF)
    blocks_in = weight_in.reshape(D, owners, HID_DEV).transpose(1, 0, 2)
    blocks_out = weight_out.reshape(D, owners, HID_DEV).transpose(1, 0, 2)
    inputs_split = pool_inputs.reshape(owners, POOL, D)
    targets_split = pool_targets.reshape(owners, POOL, D)
    picks_split = row_picks[first_turn:first_turn + STEPS].reshape(STEPS, owners, BATCH).transpose(1, 0, 2)

    def subnet(packed):
        layer_in, layer_out, rows_pool, goals_pool, chosen = packed
        for turn_index in range(STEPS):
            batch_rows = jnp.take(rows_pool, chosen[turn_index], axis=0)
            batch_goals = jnp.take(goals_pool, chosen[turn_index], axis=0)
            layer_in, layer_out = train_step(layer_in, layer_out, batch_rows, batch_goals, scale_in, scale_out)
        return (layer_in, layer_out)
    new_in, new_out = lax.map(subnet, (blocks_in, blocks_out, inputs_split, targets_split, picks_split))
    return (new_in.transpose(1, 0, 2).reshape(D, FF), new_out.transpose(1, 0, 2).reshape(D, FF))

def reference(pool_inputs, pool_targets, row_picks, weight_in, weight_out, eval_inputs, handover):
    scale_in = 1.0 / math.sqrt(D)
    scale_out = 1.0 / math.sqrt(FF)
    middle_in, middle_out = run_round(weight_in, weight_out, pool_inputs, pool_targets, row_picks, 0)
    eval_act = gelu_value(jnp.dot(eval_inputs, middle_in.astype(jnp.bfloat16), preferred_element_type=jnp.float32) * scale_in).astype(jnp.bfloat16)
    prediction = jnp.dot(eval_act, middle_out.astype(jnp.bfloat16).T, preferred_element_type=jnp.float32) * scale_out
    inverse = jnp.zeros((GROUPS,), jnp.int32).at[handover].set(jnp.arange(GROUPS, dtype=jnp.int32))
    columns = (inverse[:, None] * GROUP + jnp.arange(GROUP, dtype=jnp.int32)[None, :]).reshape(-1)
    handed_in = jnp.take(middle_in, columns, axis=1)
    handed_out = jnp.take(middle_out, columns, axis=1)
    trained_in, trained_out = run_round(handed_in, handed_out, pool_inputs, pool_targets, row_picks, STEPS)
    return (trained_in, trained_out, prediction)
```

```python
import math

import jax
import jax.numpy as jnp
from jax import lax
from jax.experimental import pallas as pl
from jax.experimental.pallas import tpu as pltpu
from jax.sharding import PartitionSpec as P

D = 4096
GROUP = 8
STEPS = 4
CHUNK = 512


tanh_coef = 0.7978845608028654
cubic_coef = 0.044715
step_rate = 0.5


def gelu_value(inputs):
    inner_term = tanh_coef * (inputs + cubic_coef * inputs * inputs * inputs)
    return 0.5 * inputs * (1.0 + jnp.tanh(inner_term))


def gelu_parts(inputs):
    tanh_part = jnp.tanh(tanh_coef * (inputs + cubic_coef * inputs * inputs * inputs))
    values = 0.5 * inputs * (1.0 + tanh_part)
    slopes = 0.5 * (1.0 + tanh_part) + 0.5 * inputs * (1.0 - tanh_part * tanh_part) * tanh_coef * (
        1.0 + 3.0 * cubic_coef * inputs * inputs
    )
    return (values, slopes)


NT = (((1,), (1,)), ((), ()))


def round_body(scale_in, scale_out, picks_ref, pin_ref, ptg_ref, wi0_ref, wo0_ref, wi_ref, wo_ref, rows_ref):
    wi_ref[...] = wi0_ref[...]
    wo_ref[...] = wo0_ref[...]
    batch = picks_ref.shape[0]
    pool = pin_ref.shape[0]
    hidden = wi_ref.shape[0]
    chunks = pin_ref.shape[1] // CHUNK
    for turn in range(picks_ref.shape[1]):
        picked = picks_ref[:, turn : turn + 1]
        onehot = (picked == lax.broadcasted_iota(jnp.int32, (batch, pool), 1)).astype(jnp.bfloat16)

        def pass_rows(c, before):
            cols = pl.ds(pl.multiple_of(c * CHUNK, CHUNK), CHUNK)
            rows_c = jnp.dot(onehot, pin_ref[:, cols], preferred_element_type=jnp.float32).astype(
                jnp.bfloat16
            )
            rows_ref[:, cols] = rows_c
            in_half = wi_ref[:, cols].astype(jnp.bfloat16)
            return before + lax.dot_general(rows_c, in_half, NT, preferred_element_type=jnp.float32)

        before = lax.fori_loop(
            0, chunks, pass_rows, jnp.zeros((batch, hidden), jnp.float32)
        ) * scale_in
        values, slopes = gelu_parts(before)
        activity = values.astype(jnp.bfloat16)
        activity_t = values.T.astype(jnp.bfloat16)

        def pass_out(c, back):
            cols = pl.ds(pl.multiple_of(c * CHUNK, CHUNK), CHUNK)
            goals_c = jnp.dot(onehot, ptg_ref[:, cols], preferred_element_type=jnp.float32)
            out_half = wo_ref[:, cols].astype(jnp.bfloat16)
            branch_c = jnp.dot(activity, out_half, preferred_element_type=jnp.float32) * scale_out
            errors_c = (branch_c - goals_c).astype(jnp.bfloat16)
            back = back + lax.dot_general(errors_c, out_half, NT, preferred_element_type=jnp.float32)
            grad_c = jnp.dot(activity_t, errors_c, preferred_element_type=jnp.float32) * scale_out
            wo_ref[:, cols] = wo_ref[:, cols] - step_rate * grad_c
            return back

        back = lax.fori_loop(0, chunks, pass_out, jnp.zeros((batch, hidden), jnp.float32))
        backward = back * scale_out * slopes
        backward_t = backward.astype(jnp.bfloat16).astype(jnp.float32).T.astype(jnp.bfloat16)

        def pass_in(c, carry):
            cols = pl.ds(pl.multiple_of(c * CHUNK, CHUNK), CHUNK)
            grad_c = jnp.dot(backward_t, rows_ref[:, cols], preferred_element_type=jnp.float32) * scale_in
            wi_ref[:, cols] = wi_ref[:, cols] - step_rate * grad_c
            return carry

        lax.fori_loop(0, chunks, pass_in, 0)


def train_round(wi_t, wo_t, pool_inputs, pool_targets, picks_t, scale_in, scale_out):
    hidden, width = wi_t.shape
    batch, turns = picks_t.shape
    pool = pool_inputs.shape[0]
    flops = turns * 2 * (2 * batch * pool * width + 5 * batch * hidden * width)
    bytes_accessed = 4 * hidden * width * 4 + 2 * pool * width * 2
    vmem = pl.BlockSpec(memory_space=pltpu.VMEM)
    return pl.pallas_call(
        lambda *refs: round_body(scale_in, scale_out, *refs),
        out_shape=(
            jax.ShapeDtypeStruct((hidden, width), jnp.float32),
            jax.ShapeDtypeStruct((hidden, width), jnp.float32),
        ),
        in_specs=[vmem] * 5,
        out_specs=(vmem, vmem),
        scratch_shapes=[pltpu.VMEM((batch, width), jnp.bfloat16)],
        compiler_params=pltpu.CompilerParams(vmem_limit_bytes=60 * 1024 * 1024),
        cost_estimate=pl.CostEstimate(
            flops=flops, transcendentals=turns * batch * hidden, bytes_accessed=bytes_accessed
        ),
        name="train_round",
    )(picks_t, pool_inputs, pool_targets, wi_t, wo_t)


def per_device(pool_inputs, pool_targets, row_picks, weight_in, weight_out, eval_inputs, handover):
    owners = lax.axis_size("sub")
    my_index = lax.axis_index("sub")
    hidden = weight_in.shape[1]
    group_count = hidden // GROUP
    scale_in = 1.0 / math.sqrt(D)
    scale_out = 1.0 / math.sqrt(hidden * owners)
    eval_all = lax.all_gather(eval_inputs, "sub", axis=0, tiled=True)
    picks_t = row_picks.T
    wi_t, wo_t = train_round(
        weight_in.T, weight_out.T, pool_inputs, pool_targets, picks_t[:, :STEPS], scale_in, scale_out
    )
    in_half = wi_t.astype(jnp.bfloat16)
    out_half = wo_t.astype(jnp.bfloat16)
    eval_act = gelu_value(
        lax.dot_general(eval_all, in_half, NT, preferred_element_type=jnp.float32) * scale_in
    ).astype(jnp.bfloat16)
    partial = jnp.dot(eval_act, out_half, preferred_element_type=jnp.float32) * scale_out
    rows_each = partial.shape[0] // owners
    gathered = lax.all_to_all(
        partial.reshape(owners, rows_each, partial.shape[1]), "sub", 0, 0, tiled=True
    )
    prediction = jnp.sum(gathered, axis=0)

    local_groups = lax.dynamic_slice_in_dim(handover, my_index * group_count, group_count, 0)
    targets = local_groups // group_count
    matches = targets[None, :] == jnp.arange(owners, dtype=jnp.int32)[:, None]
    chosen_group = jnp.sum(
        jnp.where(matches, jnp.arange(group_count, dtype=jnp.int32)[None, :], 0), axis=1
    )
    width = wi_t.shape[1]
    stacked = jnp.concatenate(
        [
            in_half.reshape(group_count, GROUP, width),
            out_half.reshape(group_count, GROUP, width),
        ],
        axis=1,
    )
    outgoing = jnp.take(stacked, chosen_group, axis=0)
    landed = lax.all_to_all(outgoing, "sub", 0, 0, tiled=True)
    positions = my_index * group_count + jnp.arange(group_count, dtype=jnp.int32)
    arriving_match = handover[None, :] == positions[:, None]
    arriving = jnp.sum(
        jnp.where(arriving_match, jnp.arange(handover.shape[0], dtype=jnp.int32)[None, :], 0), axis=1
    )
    sources = arriving // group_count
    handed = jnp.take(landed, sources, axis=0)
    handed_in = handed[:, :GROUP].reshape(hidden, width).astype(jnp.float32)
    handed_out = handed[:, GROUP:].reshape(hidden, width).astype(jnp.float32)
    trained_in, trained_out = train_round(
        handed_in, handed_out, pool_inputs, pool_targets, picks_t[:, STEPS:], scale_in, scale_out
    )
    return (trained_in.T, trained_out.T, prediction)


def solution(mesh):
    in_specs = (
        P("sub", None),
        P("sub", None),
        P(None, "sub"),
        P(None, "sub"),
        P(None, "sub"),
        P("sub", None),
        P(),
    )
    out_specs = (P(None, "sub"), P(None, "sub"), P("sub", None))
    return jax.shard_map(
        per_device, mesh=mesh, in_specs=in_specs, out_specs=out_specs, check_vma=False
    )
```

```python
import math

import jax
import jax.numpy as jnp
from jax import lax
from jax.experimental import pallas as pl
from jax.experimental.pallas import tpu as pltpu
from jax.sharding import PartitionSpec as P

D = 4096
GROUP = 8
STEPS = 4


tanh_coef = 0.7978845608028654
cubic_coef = 0.044715
step_rate = 0.5


def gelu_value(inputs):
    inner_term = tanh_coef * (inputs + cubic_coef * inputs * inputs * inputs)
    return 0.5 * inputs * (1.0 + jnp.tanh(inner_term))


def gelu_parts(inputs):
    tanh_part = jnp.tanh(tanh_coef * (inputs + cubic_coef * inputs * inputs * inputs))
    values = 0.5 * inputs * (1.0 + tanh_part)
    slopes = 0.5 * (1.0 + tanh_part) + 0.5 * inputs * (1.0 - tanh_part * tanh_part) * tanh_coef * (
        1.0 + 3.0 * cubic_coef * inputs * inputs
    )
    return (values, slopes)


NT = (((1,), (1,)), ((), ()))


def train_steps(scale_in, scale_out, picks_ref, pin_ref, ptg_ref, wi_ref, wo_ref, rows_ref):
    batch = picks_ref.shape[0]
    pool = pin_ref.shape[0]
    for turn in range(picks_ref.shape[1]):
        picked = picks_ref[:, turn : turn + 1]
        onehot = (picked == lax.broadcasted_iota(jnp.int32, (batch, pool), 1)).astype(jnp.bfloat16)
        rows = jnp.dot(onehot, pin_ref[...], preferred_element_type=jnp.float32).astype(jnp.bfloat16)
        rows_ref[...] = rows
        in_half = wi_ref[...].astype(jnp.bfloat16)
        before = lax.dot_general(rows, in_half, NT, preferred_element_type=jnp.float32) * scale_in
        values, slopes = gelu_parts(before)
        activity = values.astype(jnp.bfloat16)
        activity_t = values.T.astype(jnp.bfloat16)
        goals = jnp.dot(onehot, ptg_ref[...], preferred_element_type=jnp.float32)
        out_half = wo_ref[...].astype(jnp.bfloat16)
        branch = jnp.dot(activity, out_half, preferred_element_type=jnp.float32) * scale_out
        errors = (branch - goals).astype(jnp.bfloat16)
        back = lax.dot_general(errors, out_half, NT, preferred_element_type=jnp.float32)
        grad_out = jnp.dot(activity_t, errors, preferred_element_type=jnp.float32) * scale_out
        wo_ref[...] = wo_ref[...] - step_rate * grad_out
        backward = back * scale_out * slopes
        backward_t = backward.astype(jnp.bfloat16).astype(jnp.float32).T.astype(jnp.bfloat16)
        grad_in = jnp.dot(backward_t, rows_ref[...], preferred_element_type=jnp.float32) * scale_in
        wi_ref[...] = wi_ref[...] - step_rate * grad_in


def first_body(scale_in, scale_out, dest_ref, picks_ref, pin_ref, ptg_ref, wi0_ref, wo0_ref,
               inh_ref, outh_ref, send_ref, wi_ref, wo_ref, rows_ref, stage_ref, sems):
    wi_ref[...] = wi0_ref[...].T
    wo_ref[...] = wo0_ref[...].T
    train_steps(scale_in, scale_out, picks_ref, pin_ref, ptg_ref, wi_ref, wo_ref, rows_ref)
    inh_ref[...] = wi_ref[...].astype(jnp.bfloat16)
    outh_ref[...] = wo_ref[...].astype(jnp.bfloat16)
    groups = stage_ref.shape[0]
    for g in range(groups):
        part = pl.ds(g * GROUP, GROUP)
        stage_ref[g] = jnp.concatenate([wi_ref[part, :], wo_ref[part, :]], axis=0).astype(jnp.bfloat16)
    copies = []
    for g in range(groups):
        copy = pltpu.make_async_copy(stage_ref.at[g], send_ref.at[dest_ref[g]], sems.at[g])
        copy.start()
        copies.append(copy)
    for copy in copies:
        copy.wait()


def second_body(scale_in, scale_out, src_ref, picks_ref, pin_ref, ptg_ref, land_ref,
                ti_ref, to_ref, wi_ref, wo_ref, rows_ref, stage_ref, sems):
    groups = stage_ref.shape[0]
    copies = []
    for g in range(groups):
        copy = pltpu.make_async_copy(land_ref.at[src_ref[g]], stage_ref.at[g], sems.at[g])
        copy.start()
        copies.append(copy)
    for g in range(groups):
        copies[g].wait()
        block = stage_ref[g].astype(jnp.float32)
        part = pl.ds(g * GROUP, GROUP)
        wi_ref[part, :] = block[:GROUP]
        wo_ref[part, :] = block[GROUP:]
    train_steps(scale_in, scale_out, picks_ref, pin_ref, ptg_ref, wi_ref, wo_ref, rows_ref)
    ti_ref[...] = wi_ref[...].T
    to_ref[...] = wo_ref[...].T


def round_cost(hidden, width, batch, turns, pool):
    flops = turns * 2 * (2 * batch * pool * width + 5 * batch * hidden * width)
    return pl.CostEstimate(
        flops=flops,
        transcendentals=turns * batch * hidden,
        bytes_accessed=4 * hidden * width * 4 + 2 * pool * width * 2,
    )


VMEM_LIMIT = 63 * 1024 * 1024


def first_round(dests, picks_t, pool_inputs, pool_targets, weight_in, weight_out, owners, scale_in, scale_out):
    width, hidden = weight_in.shape
    batch, turns = picks_t.shape
    pool = pool_inputs.shape[0]
    groups = hidden // GROUP
    vmem = pl.BlockSpec(memory_space=pltpu.VMEM)
    return pl.pallas_call(
        lambda *refs: first_body(scale_in, scale_out, *refs),
        out_shape=(
            jax.ShapeDtypeStruct((hidden, width), jnp.bfloat16),
            jax.ShapeDtypeStruct((hidden, width), jnp.bfloat16),
            jax.ShapeDtypeStruct((owners, 2 * GROUP, width), jnp.bfloat16),
        ),
        in_specs=[pl.BlockSpec(memory_space=pltpu.SMEM)] + [vmem] * 5,
        out_specs=(vmem, vmem, pl.BlockSpec(memory_space=pl.ANY)),
        scratch_shapes=[
            pltpu.VMEM((hidden, width), jnp.float32),
            pltpu.VMEM((hidden, width), jnp.float32),
            pltpu.VMEM((batch, width), jnp.bfloat16),
            pltpu.VMEM((groups, 2 * GROUP, width), jnp.bfloat16),
            pltpu.SemaphoreType.DMA((groups,)),
        ],
        compiler_params=pltpu.CompilerParams(vmem_limit_bytes=VMEM_LIMIT),
        cost_estimate=round_cost(hidden, width, batch, turns, pool),
        name="first_round",
    )(dests, picks_t, pool_inputs, pool_targets, weight_in, weight_out)


def second_round(sources, picks_t, pool_inputs, pool_targets, landed, hidden, scale_in, scale_out):
    owners, _, width = landed.shape
    batch, turns = picks_t.shape
    pool = pool_inputs.shape[0]
    groups = hidden // GROUP
    vmem = pl.BlockSpec(memory_space=pltpu.VMEM)
    return pl.pallas_call(
        lambda *refs: second_body(scale_in, scale_out, *refs),
        out_shape=(
            jax.ShapeDtypeStruct((width, hidden), jnp.float32),
            jax.ShapeDtypeStruct((width, hidden), jnp.float32),
        ),
        in_specs=[pl.BlockSpec(memory_space=pltpu.SMEM), vmem, vmem, vmem,
                  pl.BlockSpec(memory_space=pl.ANY)],
        out_specs=(vmem, vmem),
        scratch_shapes=[
            pltpu.VMEM((hidden, width), jnp.float32),
            pltpu.VMEM((hidden, width), jnp.float32),
            pltpu.VMEM((batch, width), jnp.bfloat16),
            pltpu.VMEM((groups, 2 * GROUP, width), jnp.bfloat16),
            pltpu.SemaphoreType.DMA((groups,)),
        ],
        compiler_params=pltpu.CompilerParams(vmem_limit_bytes=VMEM_LIMIT),
        cost_estimate=round_cost(hidden, width, batch, turns, pool),
        name="second_round",
    )(sources, picks_t, pool_inputs, pool_targets, landed)


def per_device(pool_inputs, pool_targets, row_picks, weight_in, weight_out, eval_inputs, handover):
    owners = lax.axis_size("sub")
    my_index = lax.axis_index("sub")
    hidden = weight_in.shape[1]
    group_count = hidden // GROUP
    scale_in = 1.0 / math.sqrt(D)
    scale_out = 1.0 / math.sqrt(hidden * owners)
    eval_all = lax.all_gather(eval_inputs, "sub", axis=0, tiled=True)
    picks_t = row_picks.T
    local_groups = lax.dynamic_slice_in_dim(handover, my_index * group_count, group_count, 0)
    dests = local_groups // group_count
    in_half, out_half, outgoing = first_round(
        dests, picks_t[:, :STEPS], pool_inputs, pool_targets, weight_in, weight_out, owners,
        scale_in, scale_out,
    )
    eval_act = gelu_value(
        lax.dot_general(eval_all, in_half, NT, preferred_element_type=jnp.float32) * scale_in
    ).astype(jnp.bfloat16)
    partial = jnp.dot(eval_act, out_half, preferred_element_type=jnp.float32) * scale_out
    rows_each = partial.shape[0] // owners
    gathered = lax.all_to_all(
        partial.reshape(owners, rows_each, partial.shape[1]), "sub", 0, 0, tiled=True
    )
    prediction = jnp.sum(gathered, axis=0)

    landed = lax.all_to_all(outgoing, "sub", 0, 0, tiled=True)
    positions = my_index * group_count + jnp.arange(group_count, dtype=jnp.int32)
    arriving_match = handover[None, :] == positions[:, None]
    arriving = jnp.sum(
        jnp.where(arriving_match, jnp.arange(handover.shape[0], dtype=jnp.int32)[None, :], 0), axis=1
    )
    sources = arriving // group_count
    trained_in, trained_out = second_round(
        sources, picks_t[:, STEPS:], pool_inputs, pool_targets, landed, hidden, scale_in, scale_out
    )
    return (trained_in, trained_out, prediction)


def solution(mesh):
    in_specs = (
        P("sub", None),
        P("sub", None),
        P(None, "sub"),
        P(None, "sub"),
        P(None, "sub"),
        P("sub", None),
        P(),
    )
    out_specs = (P(None, "sub"), P(None, "sub"), P("sub", None))
    return jax.shard_map(
        per_device, mesh=mesh, in_specs=in_specs, out_specs=out_specs, check_vma=False
    )
```

```python
import math

import jax
import jax.numpy as jnp
from jax import lax
from jax.experimental import pallas as pl
from jax.experimental.pallas import tpu as pltpu
from jax.sharding import PartitionSpec as P

D = 4096
GROUP = 8
STEPS = 4


tanh_coef = 0.7978845608028654
cubic_coef = 0.044715
step_rate = 0.5


def gelu_value(inputs):
    inner_term = tanh_coef * (inputs + cubic_coef * inputs * inputs * inputs)
    return 0.5 * inputs * (1.0 + jnp.tanh(inner_term))


def gelu_parts(inputs):
    tanh_part = jnp.tanh(tanh_coef * (inputs + cubic_coef * inputs * inputs * inputs))
    values = 0.5 * inputs * (1.0 + tanh_part)
    slopes = 0.5 * (1.0 + tanh_part) + 0.5 * inputs * (1.0 - tanh_part * tanh_part) * tanh_coef * (
        1.0 + 3.0 * cubic_coef * inputs * inputs
    )
    return (values, slopes)


NT = (((1,), (1,)), ((), ()))


def train_steps(scale_in, scale_out, picks_ref, pin_ref, ptg_ref, wi_ref, wo_ref, rows_ref):
    batch = picks_ref.shape[0]
    pool = pin_ref.shape[0]
    for turn in range(picks_ref.shape[1]):
        picked = picks_ref[:, turn : turn + 1]
        onehot = (picked == lax.broadcasted_iota(jnp.int32, (batch, pool), 1)).astype(jnp.bfloat16)
        rows = jnp.dot(onehot, pin_ref[...], preferred_element_type=jnp.float32).astype(jnp.bfloat16)
        rows_ref[...] = rows
        in_half = wi_ref[...].astype(jnp.bfloat16)
        before = lax.dot_general(rows, in_half, NT, preferred_element_type=jnp.float32) * scale_in
        values, slopes = gelu_parts(before)
        activity = values.astype(jnp.bfloat16)
        activity_t = values.T.astype(jnp.bfloat16)
        goals = jnp.dot(onehot, ptg_ref[...], preferred_element_type=jnp.float32)
        out_half = wo_ref[...].astype(jnp.bfloat16)
        branch = jnp.dot(activity, out_half, preferred_element_type=jnp.float32) * scale_out
        errors = (branch - goals).astype(jnp.bfloat16)
        back = lax.dot_general(errors, out_half, NT, preferred_element_type=jnp.float32)
        grad_out = jnp.dot(activity_t, errors, preferred_element_type=jnp.float32) * scale_out
        wo_ref[...] = wo_ref[...] - step_rate * grad_out
        backward = back * scale_out * slopes
        backward_t = backward.astype(jnp.bfloat16).astype(jnp.float32).T.astype(jnp.bfloat16)
        grad_in = jnp.dot(backward_t, rows_ref[...], preferred_element_type=jnp.float32) * scale_in
        wi_ref[...] = wi_ref[...] - step_rate * grad_in


def first_body(scale_in, scale_out, dest_ref, picks_ref, pin_ref, ptg_ref, wi0_ref, wo0_ref,
               inh_ref, outh_ref, send_ref, wi_ref, wo_ref, rows_ref, stage_ref, sems):
    wi_ref[...] = wi0_ref[...].T
    wo_ref[...] = wo0_ref[...].T
    train_steps(scale_in, scale_out, picks_ref, pin_ref, ptg_ref, wi_ref, wo_ref, rows_ref)
    inh_ref[...] = wi_ref[...].astype(jnp.bfloat16)
    outh_ref[...] = wo_ref[...].astype(jnp.bfloat16)
    groups = stage_ref.shape[0]
    for g in range(groups):
        part = pl.ds(g * GROUP, GROUP)
        stage_ref[g] = jnp.concatenate([wi_ref[part, :], wo_ref[part, :]], axis=0).astype(jnp.bfloat16)
    copies = []
    for g in range(groups):
        copy = pltpu.make_async_copy(stage_ref.at[g], send_ref.at[dest_ref[g]], sems.at[g])
        copy.start()
        copies.append(copy)
    for copy in copies:
        copy.wait()


def second_body(scale_in, scale_out, src_ref, picks_ref, pin_ref, ptg_ref, land_ref,
                ti_ref, to_ref, wi_ref, wo_ref, rows_ref, stage_ref, sems):
    groups = stage_ref.shape[0]
    copies = []
    for g in range(groups):
        copy = pltpu.make_async_copy(land_ref.at[src_ref[g]], stage_ref.at[g], sems.at[g])
        copy.start()
        copies.append(copy)
    for g in range(groups):
        copies[g].wait()
        block = stage_ref[g].astype(jnp.float32)
        part = pl.ds(g * GROUP, GROUP)
        wi_ref[part, :] = block[:GROUP]
        wo_ref[part, :] = block[GROUP:]
    train_steps(scale_in, scale_out, picks_ref, pin_ref, ptg_ref, wi_ref, wo_ref, rows_ref)
    ti_ref[...] = wi_ref[...].T
    to_ref[...] = wo_ref[...].T


def round_cost(hidden, width, batch, turns, pool):
    flops = turns * 2 * (2 * batch * pool * width + 5 * batch * hidden * width)
    return pl.CostEstimate(
        flops=flops,
        transcendentals=turns * batch * hidden,
        bytes_accessed=4 * hidden * width * 4 + 2 * pool * width * 2,
    )


VMEM_LIMIT = 63 * 1024 * 1024


def first_round(dests, picks_t, pool_inputs, pool_targets, weight_in, weight_out, owners, scale_in, scale_out):
    width, hidden = weight_in.shape
    batch, turns = picks_t.shape
    pool = pool_inputs.shape[0]
    groups = hidden // GROUP
    vmem = pl.BlockSpec(memory_space=pltpu.VMEM)
    return pl.pallas_call(
        lambda *refs: first_body(scale_in, scale_out, *refs),
        out_shape=(
            jax.ShapeDtypeStruct((hidden, width), jnp.bfloat16),
            jax.ShapeDtypeStruct((hidden, width), jnp.bfloat16),
            jax.ShapeDtypeStruct((owners, 2 * GROUP, width), jnp.bfloat16),
        ),
        in_specs=[pl.BlockSpec(memory_space=pltpu.SMEM)] + [vmem] * 5,
        out_specs=(vmem, vmem, pl.BlockSpec(memory_space=pl.ANY)),
        scratch_shapes=[
            pltpu.VMEM((hidden, width), jnp.float32),
            pltpu.VMEM((hidden, width), jnp.float32),
            pltpu.VMEM((batch, width), jnp.bfloat16),
            pltpu.VMEM((groups, 2 * GROUP, width), jnp.bfloat16),
            pltpu.SemaphoreType.DMA((groups,)),
        ],
        compiler_params=pltpu.CompilerParams(vmem_limit_bytes=VMEM_LIMIT),
        cost_estimate=round_cost(hidden, width, batch, turns, pool),
        name="first_round",
    )(dests, picks_t, pool_inputs, pool_targets, weight_in, weight_out)


def second_round(sources, picks_t, pool_inputs, pool_targets, landed, hidden, scale_in, scale_out):
    owners, _, width = landed.shape
    batch, turns = picks_t.shape
    pool = pool_inputs.shape[0]
    groups = hidden // GROUP
    vmem = pl.BlockSpec(memory_space=pltpu.VMEM)
    return pl.pallas_call(
        lambda *refs: second_body(scale_in, scale_out, *refs),
        out_shape=(
            jax.ShapeDtypeStruct((width, hidden), jnp.float32),
            jax.ShapeDtypeStruct((width, hidden), jnp.float32),
        ),
        in_specs=[pl.BlockSpec(memory_space=pltpu.SMEM), vmem, vmem, vmem,
                  pl.BlockSpec(memory_space=pl.ANY)],
        out_specs=(vmem, vmem),
        scratch_shapes=[
            pltpu.VMEM((hidden, width), jnp.float32),
            pltpu.VMEM((hidden, width), jnp.float32),
            pltpu.VMEM((batch, width), jnp.bfloat16),
            pltpu.VMEM((groups, 2 * GROUP, width), jnp.bfloat16),
            pltpu.SemaphoreType.DMA((groups,)),
        ],
        compiler_params=pltpu.CompilerParams(vmem_limit_bytes=VMEM_LIMIT),
        cost_estimate=round_cost(hidden, width, batch, turns, pool),
        name="second_round",
    )(sources, picks_t, pool_inputs, pool_targets, landed)


def per_device(pool_inputs, pool_targets, row_picks, weight_in, weight_out, eval_inputs, handover):
    owners = lax.axis_size("sub")
    my_index = lax.axis_index("sub")
    hidden = weight_in.shape[1]
    group_count = hidden // GROUP
    scale_in = 1.0 / math.sqrt(D)
    scale_out = 1.0 / math.sqrt(hidden * owners)
    eval_all = lax.all_to_all(
        jnp.broadcast_to(eval_inputs[None], (owners,) + eval_inputs.shape), "sub", 0, 0, tiled=True
    ).reshape(owners * eval_inputs.shape[0], eval_inputs.shape[1])
    picks_t = row_picks.T
    local_groups = lax.dynamic_slice_in_dim(handover, my_index * group_count, group_count, 0)
    dests = local_groups // group_count
    in_half, out_half, outgoing = first_round(
        dests, picks_t[:, :STEPS], pool_inputs, pool_targets, weight_in, weight_out, owners,
        scale_in, scale_out,
    )
    eval_act = gelu_value(
        lax.dot_general(eval_all, in_half, NT, preferred_element_type=jnp.float32) * scale_in
    ).astype(jnp.bfloat16)
    partial = jnp.dot(eval_act, out_half, preferred_element_type=jnp.float32) * scale_out
    rows_each = partial.shape[0] // owners
    parity = my_index % 2
    split = partial.reshape(owners // 2, 2, rows_each, partial.shape[1])
    mine = jnp.where(parity == 0, split[:, 0], split[:, 1])
    other = jnp.where(parity == 0, split[:, 1], split[:, 0])
    pairs = [(k, k ^ 1) for k in range(owners)]
    summed = mine + lax.ppermute(other, "sub", perm=pairs)
    same_parity = [list(range(0, owners, 2)), list(range(1, owners, 2))]
    gathered = lax.all_to_all(summed, "sub", 0, 0, tiled=True, axis_index_groups=same_parity)
    prediction = jnp.sum(gathered, axis=0)

    landed = lax.all_to_all(outgoing, "sub", 0, 0, tiled=True)
    positions = my_index * group_count + jnp.arange(group_count, dtype=jnp.int32)
    arriving_match = handover[None, :] == positions[:, None]
    arriving = jnp.sum(
        jnp.where(arriving_match, jnp.arange(handover.shape[0], dtype=jnp.int32)[None, :], 0), axis=1
    )
    sources = arriving // group_count
    trained_in, trained_out = second_round(
        sources, picks_t[:, STEPS:], pool_inputs, pool_targets, landed, hidden, scale_in, scale_out
    )
    return (trained_in, trained_out, prediction)


def solution(mesh):
    in_specs = (
        P("sub", None),
        P("sub", None),
        P(None, "sub"),
        P(None, "sub"),
        P(None, "sub"),
        P("sub", None),
        P(),
    )
    out_specs = (P(None, "sub"), P(None, "sub"), P("sub", None))
    return jax.shard_map(
        per_device, mesh=mesh, in_specs=in_specs, out_specs=out_specs, check_vma=False
    )
```

```python
import math

import jax
import jax.numpy as jnp
from jax import lax
from jax.experimental import pallas as pl
from jax.experimental.pallas import tpu as pltpu
from jax.sharding import PartitionSpec as P

D = 4096
GROUP = 8
STEPS = 4


tanh_coef = 0.7978845608028654
cubic_coef = 0.044715
step_rate = 0.5


def gelu_value(inputs):
    inner_term = tanh_coef * (inputs + cubic_coef * inputs * inputs * inputs)
    return 0.5 * inputs * (1.0 + jnp.tanh(inner_term))


def gelu_parts(inputs):
    tanh_part = jnp.tanh(tanh_coef * (inputs + cubic_coef * inputs * inputs * inputs))
    values = 0.5 * inputs * (1.0 + tanh_part)
    slopes = 0.5 * (1.0 + tanh_part) + 0.5 * inputs * (1.0 - tanh_part * tanh_part) * tanh_coef * (
        1.0 + 3.0 * cubic_coef * inputs * inputs
    )
    return (values, slopes)


NT = (((1,), (1,)), ((), ()))


def train_steps(scale_in, scale_out, picks_ref, pin_ref, ptg_ref, wi_ref, wo_ref, rows_ref):
    batch = picks_ref.shape[0]
    pool = pin_ref.shape[0]
    turns = picks_ref.shape[1]

    def one_turn(turn, carry):
        lanes = lax.broadcasted_iota(jnp.int32, (batch, turns), 1)
        picked = jnp.sum(jnp.where(lanes == turn, picks_ref[...], 0), axis=1, keepdims=True)
        onehot = (picked == lax.broadcasted_iota(jnp.int32, (batch, pool), 1)).astype(jnp.bfloat16)
        rows = jnp.dot(onehot, pin_ref[...], preferred_element_type=jnp.float32).astype(jnp.bfloat16)
        rows_ref[...] = rows
        in_half = wi_ref[...].astype(jnp.bfloat16)
        before = lax.dot_general(rows, in_half, NT, preferred_element_type=jnp.float32) * scale_in
        values, slopes = gelu_parts(before)
        activity = values.astype(jnp.bfloat16)
        activity_t = values.T.astype(jnp.bfloat16)
        goals = jnp.dot(onehot, ptg_ref[...], preferred_element_type=jnp.float32)
        out_half = wo_ref[...].astype(jnp.bfloat16)
        branch = jnp.dot(activity, out_half, preferred_element_type=jnp.float32) * scale_out
        errors = (branch - goals).astype(jnp.bfloat16)
        back = lax.dot_general(errors, out_half, NT, preferred_element_type=jnp.float32)
        grad_out = jnp.dot(activity_t, errors, preferred_element_type=jnp.float32) * scale_out
        wo_ref[...] = wo_ref[...] - step_rate * grad_out
        backward = back * scale_out * slopes
        backward_t = backward.astype(jnp.bfloat16).astype(jnp.float32).T.astype(jnp.bfloat16)
        grad_in = jnp.dot(backward_t, rows_ref[...], preferred_element_type=jnp.float32) * scale_in
        wi_ref[...] = wi_ref[...] - step_rate * grad_in
        return carry

    lax.fori_loop(0, turns, one_turn, 0)


def first_body(scale_in, scale_out, dest_ref, picks_ref, pin_ref, ptg_ref, wi0_ref, wo0_ref,
               inh_ref, outh_ref, send_ref, wi_ref, wo_ref, rows_ref, stage_ref, sems):
    wi_ref[...] = wi0_ref[...].T
    wo_ref[...] = wo0_ref[...].T
    train_steps(scale_in, scale_out, picks_ref, pin_ref, ptg_ref, wi_ref, wo_ref, rows_ref)
    inh_ref[...] = wi_ref[...].astype(jnp.bfloat16)
    outh_ref[...] = wo_ref[...].astype(jnp.bfloat16)
    groups = stage_ref.shape[0]

    def pack(g, carry):
        part = pl.ds(pl.multiple_of(g * GROUP, GROUP), GROUP)
        stage_ref[g] = jnp.concatenate([wi_ref[part, :], wo_ref[part, :]], axis=0).astype(jnp.bfloat16)
        return carry

    lax.fori_loop(0, groups, pack, 0)

    def send(g, carry):
        pltpu.make_async_copy(stage_ref.at[g], send_ref.at[dest_ref[g]], sems.at[g]).start()
        return carry

    lax.fori_loop(0, groups, send, 0)

    def finish(g, carry):
        pltpu.make_async_copy(stage_ref.at[g], send_ref.at[dest_ref[g]], sems.at[g]).wait()
        return carry

    lax.fori_loop(0, groups, finish, 0)


def second_body(scale_in, scale_out, src_ref, picks_ref, pin_ref, ptg_ref, land_ref,
                ti_ref, to_ref, wi_ref, wo_ref, rows_ref, stage_ref, sems):
    groups = stage_ref.shape[0]

    def fetch(g, carry):
        pltpu.make_async_copy(land_ref.at[src_ref[g]], stage_ref.at[g], sems.at[g]).start()
        return carry

    lax.fori_loop(0, groups, fetch, 0)

    def unpack(g, carry):
        pltpu.make_async_copy(land_ref.at[src_ref[g]], stage_ref.at[g], sems.at[g]).wait()
        block = stage_ref[g].astype(jnp.float32)
        part = pl.ds(pl.multiple_of(g * GROUP, GROUP), GROUP)
        wi_ref[part, :] = block[:GROUP]
        wo_ref[part, :] = block[GROUP:]
        return carry

    lax.fori_loop(0, groups, unpack, 0)
    train_steps(scale_in, scale_out, picks_ref, pin_ref, ptg_ref, wi_ref, wo_ref, rows_ref)
    ti_ref[...] = wi_ref[...].T
    to_ref[...] = wo_ref[...].T


def round_cost(hidden, width, batch, turns, pool):
    flops = turns * 2 * (2 * batch * pool * width + 5 * batch * hidden * width)
    return pl.CostEstimate(
        flops=flops,
        transcendentals=turns * batch * hidden,
        bytes_accessed=4 * hidden * width * 4 + 2 * pool * width * 2,
    )


VMEM_LIMIT = 63 * 1024 * 1024


def first_round(dests, picks_t, pool_inputs, pool_targets, weight_in, weight_out, owners, scale_in, scale_out):
    width, hidden = weight_in.shape
    batch, turns = picks_t.shape
    pool = pool_inputs.shape[0]
    groups = hidden // GROUP
    vmem = pl.BlockSpec(memory_space=pltpu.VMEM)
    return pl.pallas_call(
        lambda *refs: first_body(scale_in, scale_out, *refs),
        out_shape=(
            jax.ShapeDtypeStruct((hidden, width), jnp.bfloat16),
            jax.ShapeDtypeStruct((hidden, width), jnp.bfloat16),
            jax.ShapeDtypeStruct((owners, 2 * GROUP, width), jnp.bfloat16),
        ),
        in_specs=[pl.BlockSpec(memory_space=pltpu.SMEM)] + [vmem] * 5,
        out_specs=(vmem, vmem, pl.BlockSpec(memory_space=pl.ANY)),
        scratch_shapes=[
            pltpu.VMEM((hidden, width), jnp.float32),
            pltpu.VMEM((hidden, width), jnp.float32),
            pltpu.VMEM((batch, width), jnp.bfloat16),
            pltpu.VMEM((groups, 2 * GROUP, width), jnp.bfloat16),
            pltpu.SemaphoreType.DMA((groups,)),
        ],
        compiler_params=pltpu.CompilerParams(vmem_limit_bytes=VMEM_LIMIT),
        cost_estimate=round_cost(hidden, width, batch, turns, pool),
        name="first_round",
    )(dests, picks_t, pool_inputs, pool_targets, weight_in, weight_out)


def second_round(sources, picks_t, pool_inputs, pool_targets, landed, hidden, scale_in, scale_out):
    owners, _, width = landed.shape
    batch, turns = picks_t.shape
    pool = pool_inputs.shape[0]
    groups = hidden // GROUP
    vmem = pl.BlockSpec(memory_space=pltpu.VMEM)
    return pl.pallas_call(
        lambda *refs: second_body(scale_in, scale_out, *refs),
        out_shape=(
            jax.ShapeDtypeStruct((width, hidden), jnp.float32),
            jax.ShapeDtypeStruct((width, hidden), jnp.float32),
        ),
        in_specs=[pl.BlockSpec(memory_space=pltpu.SMEM), vmem, vmem, vmem,
                  pl.BlockSpec(memory_space=pl.ANY)],
        out_specs=(vmem, vmem),
        scratch_shapes=[
            pltpu.VMEM((hidden, width), jnp.float32),
            pltpu.VMEM((hidden, width), jnp.float32),
            pltpu.VMEM((batch, width), jnp.bfloat16),
            pltpu.VMEM((groups, 2 * GROUP, width), jnp.bfloat16),
            pltpu.SemaphoreType.DMA((groups,)),
        ],
        compiler_params=pltpu.CompilerParams(vmem_limit_bytes=VMEM_LIMIT),
        cost_estimate=round_cost(hidden, width, batch, turns, pool),
        name="second_round",
    )(sources, picks_t, pool_inputs, pool_targets, landed)


def per_device(pool_inputs, pool_targets, row_picks, weight_in, weight_out, eval_inputs, handover):
    owners = lax.axis_size("sub")
    my_index = lax.axis_index("sub")
    hidden = weight_in.shape[1]
    group_count = hidden // GROUP
    scale_in = 1.0 / math.sqrt(D)
    scale_out = 1.0 / math.sqrt(hidden * owners)
    eval_all = lax.all_to_all(
        jnp.broadcast_to(eval_inputs[None], (owners,) + eval_inputs.shape), "sub", 0, 0, tiled=True
    ).reshape(owners * eval_inputs.shape[0], eval_inputs.shape[1])
    picks_t = row_picks.T
    local_groups = lax.dynamic_slice_in_dim(handover, my_index * group_count, group_count, 0)
    dests = local_groups // group_count
    in_half, out_half, outgoing = first_round(
        dests, picks_t[:, :STEPS], pool_inputs, pool_targets, weight_in, weight_out, owners,
        scale_in, scale_out,
    )
    landed = lax.all_to_all(outgoing, "sub", 0, 0, tiled=True)
    in_half, out_half, landed = lax.optimization_barrier((in_half, out_half, landed))
    eval_act = gelu_value(
        lax.dot_general(eval_all, in_half, NT, preferred_element_type=jnp.float32) * scale_in
    ).astype(jnp.bfloat16)
    partial = jnp.dot(eval_act, out_half, preferred_element_type=jnp.float32) * scale_out
    rows_each = partial.shape[0] // owners
    parity = my_index % 2
    split = partial.reshape(owners // 2, 2, rows_each, partial.shape[1])
    mine = jnp.where(parity == 0, split[:, 0], split[:, 1])
    other = jnp.where(parity == 0, split[:, 1], split[:, 0])
    pairs = [(k, k ^ 1) for k in range(owners)]
    summed = mine + lax.ppermute(other, "sub", perm=pairs)
    same_parity = [list(range(0, owners, 2)), list(range(1, owners, 2))]
    gathered = lax.all_to_all(summed, "sub", 0, 0, tiled=True, axis_index_groups=same_parity)
    prediction = jnp.sum(gathered, axis=0)

    positions = my_index * group_count + jnp.arange(group_count, dtype=jnp.int32)
    arriving_match = handover[None, :] == positions[:, None]
    arriving = jnp.sum(
        jnp.where(arriving_match, jnp.arange(handover.shape[0], dtype=jnp.int32)[None, :], 0), axis=1
    )
    sources = arriving // group_count
    trained_in, trained_out = second_round(
        sources, picks_t[:, STEPS:], pool_inputs, pool_targets, landed, hidden, scale_in, scale_out
    )
    return (trained_in, trained_out, prediction)


def solution(mesh):
    in_specs = (
        P("sub", None),
        P("sub", None),
        P(None, "sub"),
        P(None, "sub"),
        P(None, "sub"),
        P("sub", None),
        P(),
    )
    out_specs = (P(None, "sub"), P(None, "sub"), P("sub", None))
    return jax.shard_map(
        per_device, mesh=mesh, in_specs=in_specs, out_specs=out_specs, check_vma=False
    )
```

```python
import math

import jax
import jax.numpy as jnp
from jax import lax
from jax.experimental import pallas as pl
from jax.experimental.pallas import tpu as pltpu
from jax.sharding import PartitionSpec as P

D = 4096
GROUP = 8
STEPS = 4


tanh_coef = 0.7978845608028654
cubic_coef = 0.044715
step_rate = 0.5


def gelu_value(inputs):
    inner_term = tanh_coef * (inputs + cubic_coef * inputs * inputs * inputs)
    return 0.5 * inputs * (1.0 + jnp.tanh(inner_term))


def gelu_parts(inputs):
    tanh_part = jnp.tanh(tanh_coef * (inputs + cubic_coef * inputs * inputs * inputs))
    values = 0.5 * inputs * (1.0 + tanh_part)
    slopes = 0.5 * (1.0 + tanh_part) + 0.5 * inputs * (1.0 - tanh_part * tanh_part) * tanh_coef * (
        1.0 + 3.0 * cubic_coef * inputs * inputs
    )
    return (values, slopes)


NT = (((1,), (1,)), ((), ()))


def train_steps(scale_in, scale_out, picks_ref, pin_ref, ptg_ref, wi_ref, wo_ref, rows_ref):
    batch = picks_ref.shape[0]
    pool = pin_ref.shape[0]
    turns = picks_ref.shape[1]

    def one_turn(turn, carry):
        lanes = lax.broadcasted_iota(jnp.int32, (batch, turns), 1)
        picked = jnp.sum(jnp.where(lanes == turn, picks_ref[...], 0), axis=1, keepdims=True)
        onehot = (picked == lax.broadcasted_iota(jnp.int32, (batch, pool), 1)).astype(jnp.bfloat16)
        rows = jnp.dot(onehot, pin_ref[...], preferred_element_type=jnp.float32).astype(jnp.bfloat16)
        rows_ref[...] = rows
        in_half = wi_ref[...].astype(jnp.bfloat16)
        before = lax.dot_general(rows, in_half, NT, preferred_element_type=jnp.float32) * scale_in
        values, slopes = gelu_parts(before)
        activity = values.astype(jnp.bfloat16)
        activity_t = values.T.astype(jnp.bfloat16)
        goals = jnp.dot(onehot, ptg_ref[...], preferred_element_type=jnp.float32)
        out_half = wo_ref[...].astype(jnp.bfloat16)
        branch = jnp.dot(activity, out_half, preferred_element_type=jnp.float32) * scale_out
        errors = (branch - goals).astype(jnp.bfloat16)
        back = lax.dot_general(errors, out_half, NT, preferred_element_type=jnp.float32)
        grad_out = jnp.dot(activity_t, errors, preferred_element_type=jnp.float32) * scale_out
        wo_ref[...] = wo_ref[...] - step_rate * grad_out
        backward = back * scale_out * slopes
        backward_t = backward.astype(jnp.bfloat16).astype(jnp.float32).T.astype(jnp.bfloat16)
        grad_in = jnp.dot(backward_t, rows_ref[...], preferred_element_type=jnp.float32) * scale_in
        wi_ref[...] = wi_ref[...] - step_rate * grad_in
        return carry

    lax.fori_loop(0, turns, one_turn, 0)


def first_body(scale_in, scale_out, dest_ref, picks_ref, pin_ref, ptg_ref, wi0_ref, wo0_ref,
               inh_ref, outh_ref, send_ref, wi_ref, wo_ref, rows_ref, stage_ref, sems):
    wi_ref[...] = wi0_ref[...].T
    wo_ref[...] = wo0_ref[...].T
    train_steps(scale_in, scale_out, picks_ref, pin_ref, ptg_ref, wi_ref, wo_ref, rows_ref)
    inh_ref[...] = wi_ref[...].astype(jnp.bfloat16)
    outh_ref[...] = wo_ref[...].astype(jnp.bfloat16)
    groups = stage_ref.shape[0]

    def pack(g, carry):
        part = pl.ds(pl.multiple_of(g * GROUP, GROUP), GROUP)
        stage_ref[g] = jnp.concatenate([wi_ref[part, :], wo_ref[part, :]], axis=0).astype(jnp.bfloat16)
        return carry

    lax.fori_loop(0, groups, pack, 0)

    def send(g, carry):
        pltpu.make_async_copy(stage_ref.at[g], send_ref.at[dest_ref[g]], sems.at[g]).start()
        return carry

    lax.fori_loop(0, groups, send, 0)

    def finish(g, carry):
        pltpu.make_async_copy(stage_ref.at[g], send_ref.at[dest_ref[g]], sems.at[g]).wait()
        return carry

    lax.fori_loop(0, groups, finish, 0)


def second_body(scale_in, scale_out, src_ref, picks_ref, pin_ref, ptg_ref, land_ref,
                ti_ref, to_ref, wi_ref, wo_ref, rows_ref, stage_ref, sems):
    groups = stage_ref.shape[0]

    def fetch(g, carry):
        pltpu.make_async_copy(land_ref.at[src_ref[g]], stage_ref.at[g], sems.at[g]).start()
        return carry

    lax.fori_loop(0, groups, fetch, 0)

    def unpack(g, carry):
        pltpu.make_async_copy(land_ref.at[src_ref[g]], stage_ref.at[g], sems.at[g]).wait()
        block = stage_ref[g].astype(jnp.float32)
        part = pl.ds(pl.multiple_of(g * GROUP, GROUP), GROUP)
        wi_ref[part, :] = block[:GROUP]
        wo_ref[part, :] = block[GROUP:]
        return carry

    lax.fori_loop(0, groups, unpack, 0)
    train_steps(scale_in, scale_out, picks_ref, pin_ref, ptg_ref, wi_ref, wo_ref, rows_ref)
    ti_ref[...] = wi_ref[...].T
    to_ref[...] = wo_ref[...].T


def round_cost(hidden, width, batch, turns, pool):
    flops = turns * 2 * (2 * batch * pool * width + 5 * batch * hidden * width)
    return pl.CostEstimate(
        flops=flops,
        transcendentals=turns * batch * hidden,
        bytes_accessed=4 * hidden * width * 4 + 2 * pool * width * 2,
    )


VMEM_LIMIT = 63 * 1024 * 1024


def first_round(dests, picks_t, pool_inputs, pool_targets, weight_in, weight_out, owners, scale_in, scale_out):
    width, hidden = weight_in.shape
    batch, turns = picks_t.shape
    pool = pool_inputs.shape[0]
    groups = hidden // GROUP
    vmem = pl.BlockSpec(memory_space=pltpu.VMEM)
    return pl.pallas_call(
        lambda *refs: first_body(scale_in, scale_out, *refs),
        out_shape=(
            jax.ShapeDtypeStruct((hidden, width), jnp.bfloat16),
            jax.ShapeDtypeStruct((hidden, width), jnp.bfloat16),
            jax.ShapeDtypeStruct((owners, 2 * GROUP, width), jnp.bfloat16),
        ),
        in_specs=[pl.BlockSpec(memory_space=pltpu.SMEM)] + [vmem] * 5,
        out_specs=(vmem, vmem, pl.BlockSpec(memory_space=pl.ANY)),
        scratch_shapes=[
            pltpu.VMEM((hidden, width), jnp.float32),
            pltpu.VMEM((hidden, width), jnp.float32),
            pltpu.VMEM((batch, width), jnp.bfloat16),
            pltpu.VMEM((groups, 2 * GROUP, width), jnp.bfloat16),
            pltpu.SemaphoreType.DMA((groups,)),
        ],
        compiler_params=pltpu.CompilerParams(vmem_limit_bytes=VMEM_LIMIT),
        cost_estimate=round_cost(hidden, width, batch, turns, pool),
        name="first_round",
    )(dests, picks_t, pool_inputs, pool_targets, weight_in, weight_out)


def second_round(sources, picks_t, pool_inputs, pool_targets, landed, hidden, scale_in, scale_out):
    owners, _, width = landed.shape
    batch, turns = picks_t.shape
    pool = pool_inputs.shape[0]
    groups = hidden // GROUP
    vmem = pl.BlockSpec(memory_space=pltpu.VMEM)
    return pl.pallas_call(
        lambda *refs: second_body(scale_in, scale_out, *refs),
        out_shape=(
            jax.ShapeDtypeStruct((width, hidden), jnp.float32),
            jax.ShapeDtypeStruct((width, hidden), jnp.float32),
        ),
        in_specs=[pl.BlockSpec(memory_space=pltpu.SMEM), vmem, vmem, vmem,
                  pl.BlockSpec(memory_space=pl.ANY)],
        out_specs=(vmem, vmem),
        scratch_shapes=[
            pltpu.VMEM((hidden, width), jnp.float32),
            pltpu.VMEM((hidden, width), jnp.float32),
            pltpu.VMEM((batch, width), jnp.bfloat16),
            pltpu.VMEM((groups, 2 * GROUP, width), jnp.bfloat16),
            pltpu.SemaphoreType.DMA((groups,)),
        ],
        compiler_params=pltpu.CompilerParams(vmem_limit_bytes=VMEM_LIMIT),
        cost_estimate=round_cost(hidden, width, batch, turns, pool),
        name="second_round",
    )(sources, picks_t, pool_inputs, pool_targets, landed)


def per_device(pool_inputs, pool_targets, row_picks, weight_in, weight_out, eval_inputs, handover):
    owners = lax.axis_size("sub")
    my_index = lax.axis_index("sub")
    hidden = weight_in.shape[1]
    group_count = hidden // GROUP
    scale_in = 1.0 / math.sqrt(D)
    scale_out = 1.0 / math.sqrt(hidden * owners)
    eval_rows = eval_inputs.shape[0]
    eval_all = (
        lax.all_gather(eval_inputs, "sub", axis=0, tiled=True)
        .reshape(owners // 2, 2, eval_rows, D)
        .transpose(1, 0, 2, 3)
        .reshape(owners * eval_rows, D)
    )
    picks_t = row_picks.T
    local_groups = lax.dynamic_slice_in_dim(handover, my_index * group_count, group_count, 0)
    dests = local_groups // group_count
    in_half, out_half, outgoing = first_round(
        dests, picks_t[:, :STEPS], pool_inputs, pool_targets, weight_in, weight_out, owners,
        scale_in, scale_out,
    )
    landed = lax.all_to_all(outgoing, "sub", 0, 0, tiled=True)
    in_half, out_half, landed = lax.optimization_barrier((in_half, out_half, landed))
    eval_act = gelu_value(
        lax.dot_general(eval_all, in_half, NT, preferred_element_type=jnp.float32) * scale_in
    ).astype(jnp.bfloat16)
    partial = jnp.dot(eval_act, out_half, preferred_element_type=jnp.float32) * scale_out
    rows_each = partial.shape[0] // owners
    parity = my_index % 2
    half = partial.shape[0] // 2
    mine = lax.dynamic_slice_in_dim(partial, parity * half, half, 0).reshape(
        owners // 2, rows_each, partial.shape[1]
    )
    other = lax.dynamic_slice_in_dim(partial, (1 - parity) * half, half, 0).reshape(
        owners // 2, rows_each, partial.shape[1]
    )
    pairs = [(k, k ^ 1) for k in range(owners)]
    summed = mine + lax.ppermute(other, "sub", perm=pairs)
    same_parity = [list(range(0, owners, 2)), list(range(1, owners, 2))]
    gathered = lax.all_to_all(summed, "sub", 0, 0, tiled=True, axis_index_groups=same_parity)
    prediction = jnp.sum(gathered, axis=0)

    positions = my_index * group_count + jnp.arange(group_count, dtype=jnp.int32)
    arriving_match = handover[None, :] == positions[:, None]
    arriving = jnp.sum(
        jnp.where(arriving_match, jnp.arange(handover.shape[0], dtype=jnp.int32)[None, :], 0), axis=1
    )
    sources = arriving // group_count
    trained_in, trained_out = second_round(
        sources, picks_t[:, STEPS:], pool_inputs, pool_targets, landed, hidden, scale_in, scale_out
    )
    return (trained_in, trained_out, prediction)


def solution(mesh):
    in_specs = (
        P("sub", None),
        P("sub", None),
        P(None, "sub"),
        P(None, "sub"),
        P(None, "sub"),
        P("sub", None),
        P(),
    )
    out_specs = (P(None, "sub"), P(None, "sub"), P("sub", None))
    return jax.shard_map(
        per_device, mesh=mesh, in_specs=in_specs, out_specs=out_specs, check_vma=False
    )
```

```python
import math

import jax
import jax.numpy as jnp
from jax import lax
from jax.experimental import pallas as pl
from jax.experimental.pallas import tpu as pltpu
from jax.sharding import PartitionSpec as P

D = 4096
GROUP = 8
STEPS = 4


tanh_coef = 0.7978845608028654
cubic_coef = 0.044715
step_rate = 0.5


def gelu_value(inputs):
    inner_term = tanh_coef * (inputs + cubic_coef * inputs * inputs * inputs)
    return 0.5 * inputs * (1.0 + jnp.tanh(inner_term))


def gelu_parts(inputs):
    tanh_part = jnp.tanh(tanh_coef * (inputs + cubic_coef * inputs * inputs * inputs))
    values = 0.5 * inputs * (1.0 + tanh_part)
    slopes = 0.5 * (1.0 + tanh_part) + 0.5 * inputs * (1.0 - tanh_part * tanh_part) * tanh_coef * (
        1.0 + 3.0 * cubic_coef * inputs * inputs
    )
    return (values, slopes)


NT = (((1,), (1,)), ((), ()))


def train_steps(scale_in, scale_out, picks_ref, pin_ref, ptg_ref, wi_ref, wo_ref, rows_ref):
    batch = picks_ref.shape[0]
    pool = pin_ref.shape[0]
    turns = picks_ref.shape[1]

    def one_turn(turn, carry):
        lanes = lax.broadcasted_iota(jnp.int32, (batch, turns), 1)
        picked = jnp.sum(jnp.where(lanes == turn, picks_ref[...], 0), axis=1, keepdims=True)
        onehot = (picked == lax.broadcasted_iota(jnp.int32, (batch, pool), 1)).astype(jnp.bfloat16)
        rows = jnp.dot(onehot, pin_ref[...], preferred_element_type=jnp.float32).astype(jnp.bfloat16)
        rows_ref[...] = rows
        in_half = wi_ref[...].astype(jnp.bfloat16)
        before = lax.dot_general(rows, in_half, NT, preferred_element_type=jnp.float32) * scale_in
        values, slopes = gelu_parts(before)
        activity = values.astype(jnp.bfloat16)
        activity_t = values.T.astype(jnp.bfloat16)
        goals = jnp.dot(onehot, ptg_ref[...], preferred_element_type=jnp.float32)
        out_half = wo_ref[...].astype(jnp.bfloat16)
        branch = jnp.dot(activity, out_half, preferred_element_type=jnp.float32) * scale_out
        errors = (branch - goals).astype(jnp.bfloat16)
        back = lax.dot_general(errors, out_half, NT, preferred_element_type=jnp.float32)
        grad_out = jnp.dot(activity_t, errors, preferred_element_type=jnp.float32) * scale_out
        wo_ref[...] = wo_ref[...] - step_rate * grad_out
        backward = back * scale_out * slopes
        backward_t = backward.astype(jnp.bfloat16).astype(jnp.float32).T.astype(jnp.bfloat16)
        grad_in = jnp.dot(backward_t, rows_ref[...], preferred_element_type=jnp.float32) * scale_in
        wi_ref[...] = wi_ref[...] - step_rate * grad_in
        return carry

    lax.fori_loop(0, turns, one_turn, 0)


def first_body(scale_in, scale_out, dest_ref, picks_ref, pin_ref, ptg_ref, wi0_ref, wo0_ref,
               inh_ref, outh_ref, send_ref, wi_ref, wo_ref, rows_ref, stage_ref, sems):
    wi_ref[...] = wi0_ref[...].T
    wo_ref[...] = wo0_ref[...].T
    train_steps(scale_in, scale_out, picks_ref, pin_ref, ptg_ref, wi_ref, wo_ref, rows_ref)
    inh_ref[...] = wi_ref[...].astype(jnp.bfloat16)
    outh_ref[...] = wo_ref[...].astype(jnp.bfloat16)
    groups = stage_ref.shape[0]

    def pack(g, carry):
        part = pl.ds(pl.multiple_of(g * GROUP, GROUP), GROUP)
        stage_ref[g] = jnp.concatenate([wi_ref[part, :], wo_ref[part, :]], axis=0).astype(jnp.bfloat16)
        return carry

    lax.fori_loop(0, groups, pack, 0)

    def send(g, carry):
        pltpu.make_async_copy(stage_ref.at[g], send_ref.at[dest_ref[g]], sems.at[g]).start()
        return carry

    lax.fori_loop(0, groups, send, 0)

    def finish(g, carry):
        pltpu.make_async_copy(stage_ref.at[g], send_ref.at[dest_ref[g]], sems.at[g]).wait()
        return carry

    lax.fori_loop(0, groups, finish, 0)


def second_body(scale_in, scale_out, src_ref, picks_ref, pin_ref, ptg_ref, land_ref,
                ti_ref, to_ref, wi_ref, wo_ref, rows_ref, stage_ref, sems):
    groups = stage_ref.shape[0]

    def fetch(g, carry):
        pltpu.make_async_copy(land_ref.at[src_ref[g]], stage_ref.at[g], sems.at[g]).start()
        return carry

    lax.fori_loop(0, groups, fetch, 0)

    def unpack(g, carry):
        pltpu.make_async_copy(land_ref.at[src_ref[g]], stage_ref.at[g], sems.at[g]).wait()
        block = stage_ref[g].astype(jnp.float32)
        part = pl.ds(pl.multiple_of(g * GROUP, GROUP), GROUP)
        wi_ref[part, :] = block[:GROUP]
        wo_ref[part, :] = block[GROUP:]
        return carry

    lax.fori_loop(0, groups, unpack, 0)
    train_steps(scale_in, scale_out, picks_ref, pin_ref, ptg_ref, wi_ref, wo_ref, rows_ref)
    ti_ref[...] = wi_ref[...].T
    to_ref[...] = wo_ref[...].T


def round_cost(hidden, width, batch, turns, pool):
    flops = turns * 2 * (2 * batch * pool * width + 5 * batch * hidden * width)
    return pl.CostEstimate(
        flops=flops,
        transcendentals=turns * batch * hidden,
        bytes_accessed=4 * hidden * width * 4 + 2 * pool * width * 2,
    )


VMEM_LIMIT = 63 * 1024 * 1024


def first_round(dests, picks_t, pool_inputs, pool_targets, weight_in, weight_out, owners, scale_in, scale_out):
    width, hidden = weight_in.shape
    batch, turns = picks_t.shape
    pool = pool_inputs.shape[0]
    groups = hidden // GROUP
    vmem = pl.BlockSpec(memory_space=pltpu.VMEM)
    return pl.pallas_call(
        lambda *refs: first_body(scale_in, scale_out, *refs),
        out_shape=(
            jax.ShapeDtypeStruct((hidden, width), jnp.bfloat16),
            jax.ShapeDtypeStruct((hidden, width), jnp.bfloat16),
            jax.ShapeDtypeStruct((owners, 2 * GROUP, width), jnp.bfloat16),
        ),
        in_specs=[pl.BlockSpec(memory_space=pltpu.SMEM)] + [vmem] * 5,
        out_specs=(vmem, vmem, pl.BlockSpec(memory_space=pl.ANY)),
        scratch_shapes=[
            pltpu.VMEM((hidden, width), jnp.float32),
            pltpu.VMEM((hidden, width), jnp.float32),
            pltpu.VMEM((batch, width), jnp.bfloat16),
            pltpu.VMEM((groups, 2 * GROUP, width), jnp.bfloat16),
            pltpu.SemaphoreType.DMA((groups,)),
        ],
        compiler_params=pltpu.CompilerParams(vmem_limit_bytes=VMEM_LIMIT),
        cost_estimate=round_cost(hidden, width, batch, turns, pool),
        name="first_round",
    )(dests, picks_t, pool_inputs, pool_targets, weight_in, weight_out)


def second_round(sources, picks_t, pool_inputs, pool_targets, landed, hidden, scale_in, scale_out):
    owners, _, width = landed.shape
    batch, turns = picks_t.shape
    pool = pool_inputs.shape[0]
    groups = hidden // GROUP
    vmem = pl.BlockSpec(memory_space=pltpu.VMEM)
    return pl.pallas_call(
        lambda *refs: second_body(scale_in, scale_out, *refs),
        out_shape=(
            jax.ShapeDtypeStruct((width, hidden), jnp.float32),
            jax.ShapeDtypeStruct((width, hidden), jnp.float32),
        ),
        in_specs=[pl.BlockSpec(memory_space=pltpu.SMEM), vmem, vmem, vmem,
                  pl.BlockSpec(memory_space=pl.ANY)],
        out_specs=(vmem, vmem),
        scratch_shapes=[
            pltpu.VMEM((hidden, width), jnp.float32),
            pltpu.VMEM((hidden, width), jnp.float32),
            pltpu.VMEM((batch, width), jnp.bfloat16),
            pltpu.VMEM((groups, 2 * GROUP, width), jnp.bfloat16),
            pltpu.SemaphoreType.DMA((groups,)),
        ],
        compiler_params=pltpu.CompilerParams(vmem_limit_bytes=VMEM_LIMIT),
        cost_estimate=round_cost(hidden, width, batch, turns, pool),
        name="second_round",
    )(sources, picks_t, pool_inputs, pool_targets, landed)


def per_device(pool_inputs, pool_targets, row_picks, weight_in, weight_out, eval_inputs, handover):
    owners = lax.axis_size("sub")
    my_index = lax.axis_index("sub")
    hidden = weight_in.shape[1]
    group_count = hidden // GROUP
    scale_in = 1.0 / math.sqrt(D)
    scale_out = 1.0 / math.sqrt(hidden * owners)
    eval_all = lax.all_to_all(
        jnp.broadcast_to(eval_inputs[None], (owners,) + eval_inputs.shape), "sub", 0, 0, tiled=True
    ).reshape(owners * eval_inputs.shape[0], eval_inputs.shape[1])
    picks_t = row_picks.T
    local_groups = lax.dynamic_slice_in_dim(handover, my_index * group_count, group_count, 0)
    dests = local_groups // group_count
    in_half, out_half, outgoing = first_round(
        dests, picks_t[:, :STEPS], pool_inputs, pool_targets, weight_in, weight_out, owners,
        scale_in, scale_out,
    )
    landed = lax.all_to_all(outgoing, "sub", 0, 0, tiled=True)
    eval_act = gelu_value(
        lax.dot_general(eval_all, in_half, NT, preferred_element_type=jnp.float32) * scale_in
    ).astype(jnp.bfloat16)
    partial = jnp.dot(eval_act, out_half, preferred_element_type=jnp.float32) * scale_out
    rows_each = partial.shape[0] // owners
    parity = my_index % 2
    split = partial.reshape(owners // 2, 2, rows_each, partial.shape[1])
    mine = jnp.where(parity == 0, split[:, 0], split[:, 1])
    other = jnp.where(parity == 0, split[:, 1], split[:, 0])
    mine, other, landed = lax.optimization_barrier((mine, other, landed))
    pairs = [(k, k ^ 1) for k in range(owners)]
    summed = mine + lax.ppermute(other, "sub", perm=pairs)
    same_parity = [list(range(0, owners, 2)), list(range(1, owners, 2))]
    gathered = lax.all_to_all(summed, "sub", 0, 0, tiled=True, axis_index_groups=same_parity)
    prediction = jnp.sum(gathered, axis=0)

    positions = my_index * group_count + jnp.arange(group_count, dtype=jnp.int32)
    arriving_match = handover[None, :] == positions[:, None]
    arriving = jnp.sum(
        jnp.where(arriving_match, jnp.arange(handover.shape[0], dtype=jnp.int32)[None, :], 0), axis=1
    )
    sources = arriving // group_count
    trained_in, trained_out = second_round(
        sources, picks_t[:, STEPS:], pool_inputs, pool_targets, landed, hidden, scale_in, scale_out
    )
    return (trained_in, trained_out, prediction)


def solution(mesh):
    in_specs = (
        P("sub", None),
        P("sub", None),
        P(None, "sub"),
        P(None, "sub"),
        P(None, "sub"),
        P("sub", None),
        P(),
    )
    out_specs = (P(None, "sub"), P(None, "sub"), P("sub", None))
    return jax.shard_map(
        per_device, mesh=mesh, in_specs=in_specs, out_specs=out_specs, check_vma=False
    )
```

```python
import math

import jax
import jax.numpy as jnp
from jax import lax
from jax.experimental import pallas as pl
from jax.experimental.pallas import tpu as pltpu
from jax.sharding import PartitionSpec as P

D = 4096
GROUP = 8
STEPS = 4


tanh_coef = 0.7978845608028654
cubic_coef = 0.044715
step_rate = 0.5


def gelu_value(inputs):
    inner_term = tanh_coef * (inputs + cubic_coef * inputs * inputs * inputs)
    return 0.5 * inputs * (1.0 + jnp.tanh(inner_term))


def gelu_parts(inputs):
    tanh_part = jnp.tanh(tanh_coef * (inputs + cubic_coef * inputs * inputs * inputs))
    values = 0.5 * inputs * (1.0 + tanh_part)
    slopes = 0.5 * (1.0 + tanh_part) + 0.5 * inputs * (1.0 - tanh_part * tanh_part) * tanh_coef * (
        1.0 + 3.0 * cubic_coef * inputs * inputs
    )
    return (values, slopes)


NT = (((1,), (1,)), ((), ()))


def train_steps(scale_in, scale_out, picks_ref, pin_ref, ptg_ref, wi_ref, wo_ref, rows_ref):
    batch = picks_ref.shape[0]
    pool = pin_ref.shape[0]
    turns = picks_ref.shape[1]

    def one_turn(turn, carry):
        lanes = lax.broadcasted_iota(jnp.int32, (batch, turns), 1)
        picked = jnp.sum(jnp.where(lanes == turn, picks_ref[...], 0), axis=1, keepdims=True)
        onehot = (picked == lax.broadcasted_iota(jnp.int32, (batch, pool), 1)).astype(jnp.bfloat16)
        rows = jnp.dot(onehot, pin_ref[...], preferred_element_type=jnp.float32).astype(jnp.bfloat16)
        rows_ref[...] = rows
        in_half = wi_ref[...].astype(jnp.bfloat16)
        before = lax.dot_general(rows, in_half, NT, preferred_element_type=jnp.float32) * scale_in
        values, slopes = gelu_parts(before)
        activity = values.astype(jnp.bfloat16)
        activity_t = values.T.astype(jnp.bfloat16)
        goals = jnp.dot(onehot, ptg_ref[...], preferred_element_type=jnp.float32)
        out_half = wo_ref[...].astype(jnp.bfloat16)
        branch = jnp.dot(activity, out_half, preferred_element_type=jnp.float32) * scale_out
        errors = (branch - goals).astype(jnp.bfloat16)
        back = lax.dot_general(errors, out_half, NT, preferred_element_type=jnp.float32)
        grad_out = jnp.dot(activity_t, errors, preferred_element_type=jnp.float32) * scale_out
        wo_ref[...] = wo_ref[...] - step_rate * grad_out
        backward = back * scale_out * slopes
        backward_t = backward.astype(jnp.bfloat16).astype(jnp.float32).T.astype(jnp.bfloat16)
        grad_in = jnp.dot(backward_t, rows_ref[...], preferred_element_type=jnp.float32) * scale_in
        wi_ref[...] = wi_ref[...] - step_rate * grad_in
        return carry

    lax.fori_loop(0, turns, one_turn, 0)


def first_body(scale_in, scale_out, picks_ref, pin_ref, ptg_ref, wi0_ref, wo0_ref,
               inh_ref, outh_ref, wi_ref, wo_ref, rows_ref):
    wi_ref[...] = wi0_ref[...].T
    wo_ref[...] = wo0_ref[...].T
    train_steps(scale_in, scale_out, picks_ref, pin_ref, ptg_ref, wi_ref, wo_ref, rows_ref)
    inh_ref[...] = wi_ref[...].astype(jnp.bfloat16)
    outh_ref[...] = wo_ref[...].astype(jnp.bfloat16)


def second_body(scale_in, scale_out, src_ref, picks_ref, pin_ref, ptg_ref, land_ref,
                ti_ref, to_ref, wi_ref, wo_ref, rows_ref, stage_ref, sems):
    groups = stage_ref.shape[0]

    def fetch(g, carry):
        pltpu.make_async_copy(land_ref.at[src_ref[g]], stage_ref.at[g], sems.at[g]).start()
        return carry

    lax.fori_loop(0, groups, fetch, 0)

    def unpack(g, carry):
        pltpu.make_async_copy(land_ref.at[src_ref[g]], stage_ref.at[g], sems.at[g]).wait()
        block = stage_ref[g].astype(jnp.float32)
        part = pl.ds(pl.multiple_of(g * GROUP, GROUP), GROUP)
        wi_ref[part, :] = block[:GROUP]
        wo_ref[part, :] = block[GROUP:]
        return carry

    lax.fori_loop(0, groups, unpack, 0)
    train_steps(scale_in, scale_out, picks_ref, pin_ref, ptg_ref, wi_ref, wo_ref, rows_ref)
    ti_ref[...] = wi_ref[...].T
    to_ref[...] = wo_ref[...].T


def round_cost(hidden, width, batch, turns, pool):
    flops = turns * 2 * (2 * batch * pool * width + 5 * batch * hidden * width)
    return pl.CostEstimate(
        flops=flops,
        transcendentals=turns * batch * hidden,
        bytes_accessed=4 * hidden * width * 4 + 2 * pool * width * 2,
    )


VMEM_LIMIT = 63 * 1024 * 1024


def first_round(picks_t, pool_inputs, pool_targets, weight_in, weight_out, scale_in, scale_out):
    width, hidden = weight_in.shape
    batch, turns = picks_t.shape
    pool = pool_inputs.shape[0]
    vmem = pl.BlockSpec(memory_space=pltpu.VMEM)
    return pl.pallas_call(
        lambda *refs: first_body(scale_in, scale_out, *refs),
        out_shape=(
            jax.ShapeDtypeStruct((hidden, width), jnp.bfloat16),
            jax.ShapeDtypeStruct((hidden, width), jnp.bfloat16),
        ),
        in_specs=[vmem] * 5,
        out_specs=(vmem, vmem),
        scratch_shapes=[
            pltpu.VMEM((hidden, width), jnp.float32),
            pltpu.VMEM((hidden, width), jnp.float32),
            pltpu.VMEM((batch, width), jnp.bfloat16),
        ],
        compiler_params=pltpu.CompilerParams(vmem_limit_bytes=VMEM_LIMIT),
        cost_estimate=round_cost(hidden, width, batch, turns, pool),
        name="first_round",
    )(picks_t, pool_inputs, pool_targets, weight_in, weight_out)


def second_round(sources, picks_t, pool_inputs, pool_targets, landed, hidden, scale_in, scale_out):
    _, _, width = landed.shape
    batch, turns = picks_t.shape
    pool = pool_inputs.shape[0]
    groups = hidden // GROUP
    vmem = pl.BlockSpec(memory_space=pltpu.VMEM)
    return pl.pallas_call(
        lambda *refs: second_body(scale_in, scale_out, *refs),
        out_shape=(
            jax.ShapeDtypeStruct((width, hidden), jnp.float32),
            jax.ShapeDtypeStruct((width, hidden), jnp.float32),
        ),
        in_specs=[pl.BlockSpec(memory_space=pltpu.SMEM), vmem, vmem, vmem,
                  pl.BlockSpec(memory_space=pl.ANY)],
        out_specs=(vmem, vmem),
        scratch_shapes=[
            pltpu.VMEM((hidden, width), jnp.float32),
            pltpu.VMEM((hidden, width), jnp.float32),
            pltpu.VMEM((batch, width), jnp.bfloat16),
            pltpu.VMEM((groups, 2 * GROUP, width), jnp.bfloat16),
            pltpu.SemaphoreType.DMA((groups,)),
        ],
        compiler_params=pltpu.CompilerParams(vmem_limit_bytes=VMEM_LIMIT),
        cost_estimate=round_cost(hidden, width, batch, turns, pool),
        name="second_round",
    )(sources, picks_t, pool_inputs, pool_targets, landed)


def per_device(pool_inputs, pool_targets, row_picks, weight_in, weight_out, eval_inputs, handover):
    owners = lax.axis_size("sub")
    my_index = lax.axis_index("sub")
    hidden = weight_in.shape[1]
    group_count = hidden // GROUP
    scale_in = 1.0 / math.sqrt(D)
    scale_out = 1.0 / math.sqrt(hidden * owners)
    eval_all = lax.all_to_all(
        jnp.broadcast_to(eval_inputs[None], (owners,) + eval_inputs.shape), "sub", 0, 0, tiled=True
    ).reshape(owners * eval_inputs.shape[0], eval_inputs.shape[1])
    picks_t = row_picks.T
    in_half, out_half = first_round(
        picks_t[:, :STEPS], pool_inputs, pool_targets, weight_in, weight_out, scale_in, scale_out
    )
    pieces = owners
    piece = 2 * GROUP * D // pieces
    splits = pieces // (2 * GROUP)
    stacked = jnp.concatenate(
        [in_half.reshape(group_count, GROUP, D), out_half.reshape(group_count, GROUP, D)], axis=1
    )
    spread = (
        stacked.reshape(group_count, 2 * GROUP, splits, piece)
        .transpose(1, 2, 0, 3)
        .reshape(pieces, group_count, piece)
    )
    held = lax.all_to_all(spread, "sub", 0, 0, tiled=True).reshape(owners * group_count, piece)
    total_groups = owners * group_count
    inverse = (
        jnp.zeros((total_groups,), jnp.int32)
        .at[handover]
        .set(jnp.arange(total_groups, dtype=jnp.int32))
    )
    forward = jnp.take(held, inverse, axis=0).reshape(owners, group_count, piece)
    arrived = lax.all_to_all(forward, "sub", 0, 0, tiled=True)
    landed = (
        arrived.reshape(2 * GROUP, splits, group_count, piece)
        .transpose(2, 0, 1, 3)
        .reshape(group_count, 2 * GROUP, D)
    )
    eval_act = gelu_value(
        lax.dot_general(eval_all, in_half, NT, preferred_element_type=jnp.float32) * scale_in
    ).astype(jnp.bfloat16)
    partial = jnp.dot(eval_act, out_half, preferred_element_type=jnp.float32) * scale_out
    rows_each = partial.shape[0] // owners
    parity = my_index % 2
    split = partial.reshape(owners // 2, 2, rows_each, partial.shape[1])
    mine = jnp.where(parity == 0, split[:, 0], split[:, 1])
    other = jnp.where(parity == 0, split[:, 1], split[:, 0])
    mine, other, landed = lax.optimization_barrier((mine, other, landed))
    pairs = [(k, k ^ 1) for k in range(owners)]
    summed = mine + lax.ppermute(other, "sub", perm=pairs)
    same_parity = [list(range(0, owners, 2)), list(range(1, owners, 2))]
    gathered = lax.all_to_all(summed, "sub", 0, 0, tiled=True, axis_index_groups=same_parity)
    prediction = jnp.sum(gathered, axis=0)

    sources = jnp.arange(group_count, dtype=jnp.int32)
    trained_in, trained_out = second_round(
        sources, picks_t[:, STEPS:], pool_inputs, pool_targets, landed, hidden, scale_in, scale_out
    )
    return (trained_in, trained_out, prediction)


def solution(mesh):
    in_specs = (
        P("sub", None),
        P("sub", None),
        P(None, "sub"),
        P(None, "sub"),
        P(None, "sub"),
        P("sub", None),
        P(),
    )
    out_specs = (P(None, "sub"), P(None, "sub"), P("sub", None))
    return jax.shard_map(
        per_device, mesh=mesh, in_specs=in_specs, out_specs=out_specs, check_vma=False
    )
```

```python
import math

import jax
import jax.numpy as jnp
from jax import lax
from jax.experimental import pallas as pl
from jax.experimental.pallas import tpu as pltpu
from jax.sharding import PartitionSpec as P

D = 4096
GROUP = 8
STEPS = 4


tanh_coef = 0.7978845608028654
cubic_coef = 0.044715
step_rate = 0.5


def gelu_value(inputs):
    inner_term = tanh_coef * (inputs + cubic_coef * inputs * inputs * inputs)
    return 0.5 * inputs * (1.0 + jnp.tanh(inner_term))


def gelu_parts(inputs):
    tanh_part = jnp.tanh(tanh_coef * (inputs + cubic_coef * inputs * inputs * inputs))
    values = 0.5 * inputs * (1.0 + tanh_part)
    slopes = 0.5 * (1.0 + tanh_part) + 0.5 * inputs * (1.0 - tanh_part * tanh_part) * tanh_coef * (
        1.0 + 3.0 * cubic_coef * inputs * inputs
    )
    return (values, slopes)


NT = (((1,), (1,)), ((), ()))


def train_steps(scale_in, scale_out, picks_ref, pin_ref, ptg_ref, wi_ref, wo_ref, rows_ref):
    batch = picks_ref.shape[0]
    pool = pin_ref.shape[0]
    turns = picks_ref.shape[1]

    def one_turn(turn, carry):
        lanes = lax.broadcasted_iota(jnp.int32, (batch, turns), 1)
        picked = jnp.sum(jnp.where(lanes == turn, picks_ref[...], 0), axis=1, keepdims=True)
        onehot = (picked == lax.broadcasted_iota(jnp.int32, (batch, pool), 1)).astype(jnp.bfloat16)
        rows = jnp.dot(onehot, pin_ref[...], preferred_element_type=jnp.float32).astype(jnp.bfloat16)
        rows_ref[...] = rows
        in_half = wi_ref[...].astype(jnp.bfloat16)
        before = lax.dot_general(rows, in_half, NT, preferred_element_type=jnp.float32) * scale_in
        values, slopes = gelu_parts(before)
        activity = values.astype(jnp.bfloat16)
        activity_t = values.T.astype(jnp.bfloat16)
        goals = jnp.dot(onehot, ptg_ref[...], preferred_element_type=jnp.float32)
        out_half = wo_ref[...].astype(jnp.bfloat16)
        branch = jnp.dot(activity, out_half, preferred_element_type=jnp.float32) * scale_out
        errors = (branch - goals).astype(jnp.bfloat16)
        back = lax.dot_general(errors, out_half, NT, preferred_element_type=jnp.float32)
        grad_out = jnp.dot(activity_t, errors, preferred_element_type=jnp.float32) * scale_out
        wo_ref[...] = wo_ref[...] - step_rate * grad_out
        backward = back * scale_out * slopes
        backward_t = backward.astype(jnp.bfloat16).astype(jnp.float32).T.astype(jnp.bfloat16)
        grad_in = jnp.dot(backward_t, rows_ref[...], preferred_element_type=jnp.float32) * scale_in
        wi_ref[...] = wi_ref[...] - step_rate * grad_in
        return carry

    lax.fori_loop(0, turns, one_turn, 0)


def first_body(scale_in, scale_out, picks_ref, pin_ref, ptg_ref, wi0_ref, wo0_ref,
               inh_ref, outh_ref, wi_ref, wo_ref, rows_ref):
    wi_ref[...] = wi0_ref[...].T
    wo_ref[...] = wo0_ref[...].T
    train_steps(scale_in, scale_out, picks_ref, pin_ref, ptg_ref, wi_ref, wo_ref, rows_ref)
    inh_ref[...] = wi_ref[...].astype(jnp.bfloat16)
    outh_ref[...] = wo_ref[...].astype(jnp.bfloat16)


def second_body(scale_in, scale_out, src_ref, picks_ref, pin_ref, ptg_ref, land_ref,
                ti_ref, to_ref, wi_ref, wo_ref, rows_ref, stage_ref, sems):
    groups = stage_ref.shape[0]

    def fetch(g, carry):
        pltpu.make_async_copy(land_ref.at[src_ref[g]], stage_ref.at[g], sems.at[g]).start()
        return carry

    lax.fori_loop(0, groups, fetch, 0)

    def unpack(g, carry):
        pltpu.make_async_copy(land_ref.at[src_ref[g]], stage_ref.at[g], sems.at[g]).wait()
        block = stage_ref[g].astype(jnp.float32)
        part = pl.ds(pl.multiple_of(g * GROUP, GROUP), GROUP)
        wi_ref[part, :] = block[:GROUP]
        wo_ref[part, :] = block[GROUP:]
        return carry

    lax.fori_loop(0, groups, unpack, 0)
    train_steps(scale_in, scale_out, picks_ref, pin_ref, ptg_ref, wi_ref, wo_ref, rows_ref)
    ti_ref[...] = wi_ref[...].T
    to_ref[...] = wo_ref[...].T


def round_cost(hidden, width, batch, turns, pool):
    flops = turns * 2 * (2 * batch * pool * width + 5 * batch * hidden * width)
    return pl.CostEstimate(
        flops=flops,
        transcendentals=turns * batch * hidden,
        bytes_accessed=4 * hidden * width * 4 + 2 * pool * width * 2,
    )


VMEM_LIMIT = 63 * 1024 * 1024


def first_round(picks_t, pool_inputs, pool_targets, weight_in, weight_out, scale_in, scale_out):
    width, hidden = weight_in.shape
    batch, turns = picks_t.shape
    pool = pool_inputs.shape[0]
    vmem = pl.BlockSpec(memory_space=pltpu.VMEM)
    return pl.pallas_call(
        lambda *refs: first_body(scale_in, scale_out, *refs),
        out_shape=(
            jax.ShapeDtypeStruct((hidden, width), jnp.bfloat16),
            jax.ShapeDtypeStruct((hidden, width), jnp.bfloat16),
        ),
        in_specs=[vmem] * 5,
        out_specs=(vmem, vmem),
        scratch_shapes=[
            pltpu.VMEM((hidden, width), jnp.float32),
            pltpu.VMEM((hidden, width), jnp.float32),
            pltpu.VMEM((batch, width), jnp.bfloat16),
        ],
        compiler_params=pltpu.CompilerParams(vmem_limit_bytes=VMEM_LIMIT),
        cost_estimate=round_cost(hidden, width, batch, turns, pool),
        name="first_round",
    )(picks_t, pool_inputs, pool_targets, weight_in, weight_out)


def second_round(sources, picks_t, pool_inputs, pool_targets, landed, hidden, scale_in, scale_out):
    _, _, width = landed.shape
    batch, turns = picks_t.shape
    pool = pool_inputs.shape[0]
    groups = hidden // GROUP
    vmem = pl.BlockSpec(memory_space=pltpu.VMEM)
    return pl.pallas_call(
        lambda *refs: second_body(scale_in, scale_out, *refs),
        out_shape=(
            jax.ShapeDtypeStruct((width, hidden), jnp.float32),
            jax.ShapeDtypeStruct((width, hidden), jnp.float32),
        ),
        in_specs=[pl.BlockSpec(memory_space=pltpu.SMEM), vmem, vmem, vmem,
                  pl.BlockSpec(memory_space=pl.ANY)],
        out_specs=(vmem, vmem),
        scratch_shapes=[
            pltpu.VMEM((hidden, width), jnp.float32),
            pltpu.VMEM((hidden, width), jnp.float32),
            pltpu.VMEM((batch, width), jnp.bfloat16),
            pltpu.VMEM((groups, 2 * GROUP, width), jnp.bfloat16),
            pltpu.SemaphoreType.DMA((groups,)),
        ],
        compiler_params=pltpu.CompilerParams(vmem_limit_bytes=VMEM_LIMIT),
        cost_estimate=round_cost(hidden, width, batch, turns, pool),
        name="second_round",
    )(sources, picks_t, pool_inputs, pool_targets, landed)


def per_device(pool_inputs, pool_targets, row_picks, weight_in, weight_out, eval_inputs, handover):
    owners = lax.axis_size("sub")
    my_index = lax.axis_index("sub")
    hidden = weight_in.shape[1]
    group_count = hidden // GROUP
    scale_in = 1.0 / math.sqrt(D)
    scale_out = 1.0 / math.sqrt(hidden * owners)
    eval_all = lax.all_to_all(
        jnp.broadcast_to(eval_inputs[None], (owners,) + eval_inputs.shape), "sub", 0, 0, tiled=True
    ).reshape(owners * eval_inputs.shape[0], eval_inputs.shape[1])
    picks_t = row_picks.T
    in_half, out_half = first_round(
        picks_t[:, :STEPS], pool_inputs, pool_targets, weight_in, weight_out, scale_in, scale_out
    )
    pieces = owners
    piece = 2 * GROUP * D // pieces
    splits = pieces // (2 * GROUP)
    stacked = jnp.concatenate(
        [in_half.reshape(group_count, GROUP, D), out_half.reshape(group_count, GROUP, D)], axis=1
    )
    spread = (
        stacked.reshape(group_count, 2 * GROUP, splits, piece)
        .transpose(1, 2, 0, 3)
        .reshape(pieces, group_count, piece)
    )
    held = lax.all_to_all(spread, "sub", 0, 0, tiled=True).reshape(owners * group_count, piece)
    forward = (
        jnp.zeros_like(held)
        .at[handover]
        .set(held, unique_indices=True)
        .reshape(owners, group_count, piece)
    )
    arrived = lax.all_to_all(forward, "sub", 0, 0, tiled=True)
    landed = (
        arrived.reshape(2 * GROUP, splits, group_count, piece)
        .transpose(2, 0, 1, 3)
        .reshape(group_count, 2 * GROUP, D)
    )
    eval_act = gelu_value(
        lax.dot_general(eval_all, in_half, NT, preferred_element_type=jnp.float32) * scale_in
    ).astype(jnp.bfloat16)
    partial = jnp.dot(eval_act, out_half, preferred_element_type=jnp.float32) * scale_out
    rows_each = partial.shape[0] // owners
    parity = my_index % 2
    split = partial.reshape(owners // 2, 2, rows_each, partial.shape[1])
    mine = jnp.where(parity == 0, split[:, 0], split[:, 1])
    other = jnp.where(parity == 0, split[:, 1], split[:, 0])
    mine, other, landed = lax.optimization_barrier((mine, other, landed))
    pairs = [(k, k ^ 1) for k in range(owners)]
    summed = mine + lax.ppermute(other, "sub", perm=pairs)
    same_parity = [list(range(0, owners, 2)), list(range(1, owners, 2))]
    gathered = lax.all_to_all(summed, "sub", 0, 0, tiled=True, axis_index_groups=same_parity)
    prediction = jnp.sum(gathered, axis=0)

    sources = jnp.arange(group_count, dtype=jnp.int32)
    trained_in, trained_out = second_round(
        sources, picks_t[:, STEPS:], pool_inputs, pool_targets, landed, hidden, scale_in, scale_out
    )
    return (trained_in, trained_out, prediction)


def solution(mesh):
    in_specs = (
        P("sub", None),
        P("sub", None),
        P(None, "sub"),
        P(None, "sub"),
        P(None, "sub"),
        P("sub", None),
        P(),
    )
    out_specs = (P(None, "sub"), P(None, "sub"), P("sub", None))
    return jax.shard_map(
        per_device, mesh=mesh, in_specs=in_specs, out_specs=out_specs, check_vma=False
    )
```

```python
import math

import jax
import jax.numpy as jnp
from jax import lax
from jax.experimental import pallas as pl
from jax.experimental.pallas import tpu as pltpu
from jax.sharding import PartitionSpec as P

D = 4096
GROUP = 8
STEPS = 4


tanh_coef = 0.7978845608028654
cubic_coef = 0.044715
step_rate = 0.5


def gelu_value(inputs):
    inner_term = tanh_coef * (inputs + cubic_coef * inputs * inputs * inputs)
    return 0.5 * inputs * (1.0 + jnp.tanh(inner_term))


def gelu_parts(inputs):
    tanh_part = jnp.tanh(tanh_coef * (inputs + cubic_coef * inputs * inputs * inputs))
    values = 0.5 * inputs * (1.0 + tanh_part)
    slopes = 0.5 * (1.0 + tanh_part) + 0.5 * inputs * (1.0 - tanh_part * tanh_part) * tanh_coef * (
        1.0 + 3.0 * cubic_coef * inputs * inputs
    )
    return (values, slopes)


NT = (((1,), (1,)), ((), ()))


def train_steps(scale_in, scale_out, picks_ref, pin_ref, ptg_ref, wi_ref, wo_ref, rows_ref):
    batch = picks_ref.shape[0]
    pool = pin_ref.shape[0]
    turns = picks_ref.shape[1]

    def one_turn(turn, carry):
        lanes = lax.broadcasted_iota(jnp.int32, (batch, turns), 1)
        picked = jnp.sum(jnp.where(lanes == turn, picks_ref[...], 0), axis=1, keepdims=True)
        onehot = (picked == lax.broadcasted_iota(jnp.int32, (batch, pool), 1)).astype(jnp.bfloat16)
        rows = jnp.dot(onehot, pin_ref[...], preferred_element_type=jnp.float32).astype(jnp.bfloat16)
        rows_ref[...] = rows
        in_half = wi_ref[...].astype(jnp.bfloat16)
        before = lax.dot_general(rows, in_half, NT, preferred_element_type=jnp.float32) * scale_in
        values, slopes = gelu_parts(before)
        activity = values.astype(jnp.bfloat16)
        activity_t = values.T.astype(jnp.bfloat16)
        goals = jnp.dot(onehot, ptg_ref[...], preferred_element_type=jnp.float32)
        out_half = wo_ref[...].astype(jnp.bfloat16)
        branch = jnp.dot(activity, out_half, preferred_element_type=jnp.float32) * scale_out
        errors = (branch - goals).astype(jnp.bfloat16)
        back = lax.dot_general(errors, out_half, NT, preferred_element_type=jnp.float32)
        grad_out = jnp.dot(activity_t, errors, preferred_element_type=jnp.float32) * scale_out
        wo_ref[...] = wo_ref[...] - step_rate * grad_out
        backward = back * scale_out * slopes
        backward_t = backward.astype(jnp.bfloat16).astype(jnp.float32).T.astype(jnp.bfloat16)
        grad_in = jnp.dot(backward_t, rows_ref[...], preferred_element_type=jnp.float32) * scale_in
        wi_ref[...] = wi_ref[...] - step_rate * grad_in
        return carry

    lax.fori_loop(0, turns, one_turn, 0)


def first_body(scale_in, scale_out, picks_ref, pin_ref, ptg_ref, wi0_ref, wo0_ref,
               inh_ref, outh_ref, wi_ref, wo_ref, rows_ref):
    wi_ref[...] = wi0_ref[...].T
    wo_ref[...] = wo0_ref[...].T
    train_steps(scale_in, scale_out, picks_ref, pin_ref, ptg_ref, wi_ref, wo_ref, rows_ref)
    inh_ref[...] = wi_ref[...].astype(jnp.bfloat16)
    outh_ref[...] = wo_ref[...].astype(jnp.bfloat16)


def second_body(scale_in, scale_out, src_ref, picks_ref, pin_ref, ptg_ref, land_ref,
                ti_ref, to_ref, wi_ref, wo_ref, rows_ref, stage_ref, sems):
    groups = stage_ref.shape[0]

    def fetch(g, carry):
        pltpu.make_async_copy(land_ref.at[src_ref[g]], stage_ref.at[g], sems.at[g]).start()
        return carry

    lax.fori_loop(0, groups, fetch, 0)

    def unpack(g, carry):
        pltpu.make_async_copy(land_ref.at[src_ref[g]], stage_ref.at[g], sems.at[g]).wait()
        block = stage_ref[g].astype(jnp.float32)
        part = pl.ds(pl.multiple_of(g * GROUP, GROUP), GROUP)
        wi_ref[part, :] = block[:GROUP]
        wo_ref[part, :] = block[GROUP:]
        return carry

    lax.fori_loop(0, groups, unpack, 0)
    train_steps(scale_in, scale_out, picks_ref, pin_ref, ptg_ref, wi_ref, wo_ref, rows_ref)
    ti_ref[...] = wi_ref[...].T
    to_ref[...] = wo_ref[...].T


def round_cost(hidden, width, batch, turns, pool):
    flops = turns * 2 * (2 * batch * pool * width + 5 * batch * hidden * width)
    return pl.CostEstimate(
        flops=flops,
        transcendentals=turns * batch * hidden,
        bytes_accessed=4 * hidden * width * 4 + 2 * pool * width * 2,
    )


VMEM_LIMIT = 63 * 1024 * 1024


def first_round(picks_t, pool_inputs, pool_targets, weight_in, weight_out, scale_in, scale_out):
    width, hidden = weight_in.shape
    batch, turns = picks_t.shape
    pool = pool_inputs.shape[0]
    vmem = pl.BlockSpec(memory_space=pltpu.VMEM)
    return pl.pallas_call(
        lambda *refs: first_body(scale_in, scale_out, *refs),
        out_shape=(
            jax.ShapeDtypeStruct((hidden, width), jnp.bfloat16),
            jax.ShapeDtypeStruct((hidden, width), jnp.bfloat16),
        ),
        in_specs=[vmem] * 5,
        out_specs=(vmem, vmem),
        scratch_shapes=[
            pltpu.VMEM((hidden, width), jnp.float32),
            pltpu.VMEM((hidden, width), jnp.float32),
            pltpu.VMEM((batch, width), jnp.bfloat16),
        ],
        compiler_params=pltpu.CompilerParams(vmem_limit_bytes=VMEM_LIMIT),
        cost_estimate=round_cost(hidden, width, batch, turns, pool),
        name="first_round",
    )(picks_t, pool_inputs, pool_targets, weight_in, weight_out)


def second_round(sources, picks_t, pool_inputs, pool_targets, landed, hidden, scale_in, scale_out):
    _, _, width = landed.shape
    batch, turns = picks_t.shape
    pool = pool_inputs.shape[0]
    groups = hidden // GROUP
    vmem = pl.BlockSpec(memory_space=pltpu.VMEM)
    return pl.pallas_call(
        lambda *refs: second_body(scale_in, scale_out, *refs),
        out_shape=(
            jax.ShapeDtypeStruct((width, hidden), jnp.float32),
            jax.ShapeDtypeStruct((width, hidden), jnp.float32),
        ),
        in_specs=[pl.BlockSpec(memory_space=pltpu.SMEM), vmem, vmem, vmem,
                  pl.BlockSpec(memory_space=pl.ANY)],
        out_specs=(vmem, vmem),
        scratch_shapes=[
            pltpu.VMEM((hidden, width), jnp.float32),
            pltpu.VMEM((hidden, width), jnp.float32),
            pltpu.VMEM((batch, width), jnp.bfloat16),
            pltpu.VMEM((groups, 2 * GROUP, width), jnp.bfloat16),
            pltpu.SemaphoreType.DMA((groups,)),
        ],
        compiler_params=pltpu.CompilerParams(vmem_limit_bytes=VMEM_LIMIT),
        cost_estimate=round_cost(hidden, width, batch, turns, pool),
        name="second_round",
    )(sources, picks_t, pool_inputs, pool_targets, landed)


def per_device(pool_inputs, pool_targets, row_picks, weight_in, weight_out, eval_inputs, handover):
    owners = lax.axis_size("sub")
    my_index = lax.axis_index("sub")
    hidden = weight_in.shape[1]
    group_count = hidden // GROUP
    scale_in = 1.0 / math.sqrt(D)
    scale_out = 1.0 / math.sqrt(hidden * owners)
    picks_t = row_picks.T
    in_half, out_half = first_round(
        picks_t[:, :STEPS], pool_inputs, pool_targets, weight_in, weight_out, scale_in, scale_out
    )
    pieces = owners
    piece = 2 * GROUP * D // pieces
    splits = pieces // (2 * GROUP)
    stacked = jnp.concatenate(
        [in_half.reshape(group_count, GROUP, D), out_half.reshape(group_count, GROUP, D)], axis=1
    )
    spread = (
        stacked.reshape(group_count, 2 * GROUP, splits, piece)
        .transpose(1, 2, 0, 3)
        .reshape(pieces, group_count, piece)
    )
    eval_rows = eval_inputs.shape[0]
    eval_pieces = eval_rows * D // piece
    eval_spread = jnp.broadcast_to(
        eval_inputs.reshape(1, eval_pieces, piece), (pieces, eval_pieces, piece)
    )
    held_all = lax.all_to_all(
        jnp.concatenate([spread, eval_spread], axis=1), "sub", 0, 0, tiled=True
    )
    held = held_all[:, :group_count].reshape(owners * group_count, piece)
    eval_all = held_all[:, group_count:].reshape(owners * eval_rows, D)
    forward = (
        jnp.zeros_like(held)
        .at[handover]
        .set(held, unique_indices=True)
        .reshape(owners, group_count, piece)
    )
    arrived = lax.all_to_all(forward, "sub", 0, 0, tiled=True)
    landed = (
        arrived.reshape(2 * GROUP, splits, group_count, piece)
        .transpose(2, 0, 1, 3)
        .reshape(group_count, 2 * GROUP, D)
    )
    eval_act = gelu_value(
        lax.dot_general(eval_all, in_half, NT, preferred_element_type=jnp.float32) * scale_in
    ).astype(jnp.bfloat16)
    partial = jnp.dot(eval_act, out_half, preferred_element_type=jnp.float32) * scale_out
    rows_each = partial.shape[0] // owners
    parity = my_index % 2
    split = partial.reshape(owners // 2, 2, rows_each, partial.shape[1])
    mine = jnp.where(parity == 0, split[:, 0], split[:, 1])
    other = jnp.where(parity == 0, split[:, 1], split[:, 0])
    mine, other, landed = lax.optimization_barrier((mine, other, landed))
    pairs = [(k, k ^ 1) for k in range(owners)]
    summed = mine + lax.ppermute(other, "sub", perm=pairs)
    same_parity = [list(range(0, owners, 2)), list(range(1, owners, 2))]
    gathered = lax.all_to_all(summed, "sub", 0, 0, tiled=True, axis_index_groups=same_parity)
    prediction = jnp.sum(gathered, axis=0)

    sources = jnp.arange(group_count, dtype=jnp.int32)
    trained_in, trained_out = second_round(
        sources, picks_t[:, STEPS:], pool_inputs, pool_targets, landed, hidden, scale_in, scale_out
    )
    return (trained_in, trained_out, prediction)


def solution(mesh):
    in_specs = (
        P("sub", None),
        P("sub", None),
        P(None, "sub"),
        P(None, "sub"),
        P(None, "sub"),
        P("sub", None),
        P(),
    )
    out_specs = (P(None, "sub"), P(None, "sub"), P("sub", None))
    return jax.shard_map(
        per_device, mesh=mesh, in_specs=in_specs, out_specs=out_specs, check_vma=False
    )
```

```python
import math

import jax
import jax.numpy as jnp
from jax import lax
from jax.experimental import pallas as pl
from jax.experimental.pallas import tpu as pltpu
from jax.sharding import PartitionSpec as P

D = 4096
GROUP = 8
STEPS = 4


tanh_coef = 0.7978845608028654
cubic_coef = 0.044715
step_rate = 0.5


def gelu_value(inputs):
    inner_term = tanh_coef * (inputs + cubic_coef * inputs * inputs * inputs)
    return 0.5 * inputs * (1.0 + jnp.tanh(inner_term))


def gelu_parts(inputs):
    tanh_part = jnp.tanh(tanh_coef * (inputs + cubic_coef * inputs * inputs * inputs))
    values = 0.5 * inputs * (1.0 + tanh_part)
    slopes = 0.5 * (1.0 + tanh_part) + 0.5 * inputs * (1.0 - tanh_part * tanh_part) * tanh_coef * (
        1.0 + 3.0 * cubic_coef * inputs * inputs
    )
    return (values, slopes)


NT = (((1,), (1,)), ((), ()))


def train_steps(scale_in, scale_out, picks_ref, pin_ref, ptg_ref, wi_ref, wo_ref, rows_ref):
    batch = picks_ref.shape[0]
    pool = pin_ref.shape[0]
    turns = picks_ref.shape[1]

    def one_turn(turn, carry):
        lanes = lax.broadcasted_iota(jnp.int32, (batch, turns), 1)
        picked = jnp.sum(jnp.where(lanes == turn, picks_ref[...], 0), axis=1, keepdims=True)
        onehot = (picked == lax.broadcasted_iota(jnp.int32, (batch, pool), 1)).astype(jnp.bfloat16)
        rows = jnp.dot(onehot, pin_ref[...], preferred_element_type=jnp.float32).astype(jnp.bfloat16)
        rows_ref[...] = rows
        in_half = wi_ref[...].astype(jnp.bfloat16)
        before = lax.dot_general(rows, in_half, NT, preferred_element_type=jnp.float32) * scale_in
        values, slopes = gelu_parts(before)
        activity = values.astype(jnp.bfloat16)
        activity_t = values.T.astype(jnp.bfloat16)
        goals = jnp.dot(onehot, ptg_ref[...], preferred_element_type=jnp.float32)
        out_half = wo_ref[...].astype(jnp.bfloat16)
        branch = jnp.dot(activity, out_half, preferred_element_type=jnp.float32) * scale_out
        errors = (branch - goals).astype(jnp.bfloat16)
        back = lax.dot_general(errors, out_half, NT, preferred_element_type=jnp.float32)
        grad_out = jnp.dot(activity_t, errors, preferred_element_type=jnp.float32) * scale_out
        wo_ref[...] = wo_ref[...] - step_rate * grad_out
        backward = back * scale_out * slopes
        backward_t = backward.astype(jnp.bfloat16).astype(jnp.float32).T.astype(jnp.bfloat16)
        grad_in = jnp.dot(backward_t, rows_ref[...], preferred_element_type=jnp.float32) * scale_in
        wi_ref[...] = wi_ref[...] - step_rate * grad_in
        return carry

    lax.fori_loop(0, turns, one_turn, 0)


def first_body(scale_in, scale_out, picks_ref, pin_ref, ptg_ref, wi0_ref, wo0_ref,
               inh_ref, outh_ref, wi_ref, wo_ref, rows_ref):
    wi_ref[...] = wi0_ref[...].T
    wo_ref[...] = wo0_ref[...].T
    train_steps(scale_in, scale_out, picks_ref, pin_ref, ptg_ref, wi_ref, wo_ref, rows_ref)
    inh_ref[...] = wi_ref[...].astype(jnp.bfloat16)
    outh_ref[...] = wo_ref[...].astype(jnp.bfloat16)


def second_body(scale_in, scale_out, src_ref, picks_ref, pin_ref, ptg_ref, land_ref,
                ti_ref, to_ref, wi_ref, wo_ref, rows_ref, stage_ref, sems):
    groups = stage_ref.shape[0]

    def fetch(g, carry):
        pltpu.make_async_copy(land_ref.at[src_ref[g]], stage_ref.at[g], sems.at[g]).start()
        return carry

    lax.fori_loop(0, groups, fetch, 0)

    def unpack(g, carry):
        pltpu.make_async_copy(land_ref.at[src_ref[g]], stage_ref.at[g], sems.at[g]).wait()
        block = stage_ref[g].astype(jnp.float32)
        part = pl.ds(pl.multiple_of(g * GROUP, GROUP), GROUP)
        wi_ref[part, :] = block[:GROUP]
        wo_ref[part, :] = block[GROUP:]
        return carry

    lax.fori_loop(0, groups, unpack, 0)
    train_steps(scale_in, scale_out, picks_ref, pin_ref, ptg_ref, wi_ref, wo_ref, rows_ref)
    ti_ref[...] = wi_ref[...].T
    to_ref[...] = wo_ref[...].T


def round_cost(hidden, width, batch, turns, pool):
    flops = turns * 2 * (2 * batch * pool * width + 5 * batch * hidden * width)
    return pl.CostEstimate(
        flops=flops,
        transcendentals=turns * batch * hidden,
        bytes_accessed=4 * hidden * width * 4 + 2 * pool * width * 2,
    )


VMEM_LIMIT = 63 * 1024 * 1024


def first_round(picks_t, pool_inputs, pool_targets, weight_in, weight_out, scale_in, scale_out):
    width, hidden = weight_in.shape
    batch, turns = picks_t.shape
    pool = pool_inputs.shape[0]
    vmem = pl.BlockSpec(memory_space=pltpu.VMEM)
    return pl.pallas_call(
        lambda *refs: first_body(scale_in, scale_out, *refs),
        out_shape=(
            jax.ShapeDtypeStruct((hidden, width), jnp.bfloat16),
            jax.ShapeDtypeStruct((hidden, width), jnp.bfloat16),
        ),
        in_specs=[vmem] * 5,
        out_specs=(vmem, vmem),
        scratch_shapes=[
            pltpu.VMEM((hidden, width), jnp.float32),
            pltpu.VMEM((hidden, width), jnp.float32),
            pltpu.VMEM((batch, width), jnp.bfloat16),
        ],
        compiler_params=pltpu.CompilerParams(vmem_limit_bytes=VMEM_LIMIT),
        cost_estimate=round_cost(hidden, width, batch, turns, pool),
        name="first_round",
    )(picks_t, pool_inputs, pool_targets, weight_in, weight_out)


def second_round(sources, picks_t, pool_inputs, pool_targets, landed, hidden, scale_in, scale_out):
    _, _, width = landed.shape
    batch, turns = picks_t.shape
    pool = pool_inputs.shape[0]
    groups = hidden // GROUP
    vmem = pl.BlockSpec(memory_space=pltpu.VMEM)
    return pl.pallas_call(
        lambda *refs: second_body(scale_in, scale_out, *refs),
        out_shape=(
            jax.ShapeDtypeStruct((width, hidden), jnp.float32),
            jax.ShapeDtypeStruct((width, hidden), jnp.float32),
        ),
        in_specs=[pl.BlockSpec(memory_space=pltpu.SMEM), vmem, vmem, vmem,
                  pl.BlockSpec(memory_space=pl.ANY)],
        out_specs=(vmem, vmem),
        scratch_shapes=[
            pltpu.VMEM((hidden, width), jnp.float32),
            pltpu.VMEM((hidden, width), jnp.float32),
            pltpu.VMEM((batch, width), jnp.bfloat16),
            pltpu.VMEM((groups, 2 * GROUP, width), jnp.bfloat16),
            pltpu.SemaphoreType.DMA((groups,)),
        ],
        compiler_params=pltpu.CompilerParams(vmem_limit_bytes=VMEM_LIMIT),
        cost_estimate=round_cost(hidden, width, batch, turns, pool),
        name="second_round",
    )(sources, picks_t, pool_inputs, pool_targets, landed)


def per_device(pool_inputs, pool_targets, row_picks, weight_in, weight_out, eval_inputs, handover):
    owners = lax.axis_size("sub")
    my_index = lax.axis_index("sub")
    hidden = weight_in.shape[1]
    group_count = hidden // GROUP
    scale_in = 1.0 / math.sqrt(D)
    scale_out = 1.0 / math.sqrt(hidden * owners)
    picks_t = row_picks.T
    in_half, out_half = first_round(
        picks_t[:, :STEPS], pool_inputs, pool_targets, weight_in, weight_out, scale_in, scale_out
    )
    pieces = owners
    piece = 2 * GROUP * D // pieces
    splits = pieces // (2 * GROUP)
    stacked = jnp.concatenate(
        [in_half.reshape(group_count, GROUP, D), out_half.reshape(group_count, GROUP, D)], axis=1
    )
    spread = (
        stacked.reshape(group_count, 2 * GROUP, splits, piece)
        .transpose(1, 2, 0, 3)
        .reshape(pieces, group_count, piece)
    )
    eval_rows = eval_inputs.shape[0]
    eval_pieces = eval_rows * D // piece
    eval_spread = jnp.broadcast_to(
        eval_inputs.reshape(1, eval_pieces, piece), (pieces, eval_pieces, piece)
    )
    held_all = lax.all_to_all(
        jnp.concatenate([spread, eval_spread], axis=1), "sub", 0, 0, tiled=True
    )
    held = held_all[:, :group_count].reshape(owners * group_count, piece)
    eval_all = held_all[:, group_count:].reshape(owners * eval_rows, D)
    total_groups = owners * group_count
    inverse = (
        jnp.zeros((total_groups,), jnp.int32)
        .at[handover]
        .set(jnp.arange(total_groups, dtype=jnp.int32))
    )
    forward = jnp.take(held, inverse, axis=0).reshape(owners, group_count, piece)
    arrived = lax.all_to_all(forward, "sub", 0, 0, tiled=True)
    landed = (
        arrived.reshape(2 * GROUP, splits, group_count, piece)
        .transpose(2, 0, 1, 3)
        .reshape(group_count, 2 * GROUP, D)
    )
    eval_act = gelu_value(
        lax.dot_general(eval_all, in_half, NT, preferred_element_type=jnp.float32) * scale_in
    ).astype(jnp.bfloat16)
    partial = jnp.dot(eval_act, out_half, preferred_element_type=jnp.float32) * scale_out
    rows_each = partial.shape[0] // owners
    parity = my_index % 2
    split = partial.reshape(owners // 2, 2, rows_each, partial.shape[1])
    mine = jnp.where(parity == 0, split[:, 0], split[:, 1])
    other = jnp.where(parity == 0, split[:, 1], split[:, 0])
    mine, other, landed = lax.optimization_barrier((mine, other, landed))
    pairs = [(k, k ^ 1) for k in range(owners)]
    summed = mine + lax.ppermute(other, "sub", perm=pairs)
    same_parity = [list(range(0, owners, 2)), list(range(1, owners, 2))]
    gathered = lax.all_to_all(summed, "sub", 0, 0, tiled=True, axis_index_groups=same_parity)
    prediction = jnp.sum(gathered, axis=0)

    sources = jnp.arange(group_count, dtype=jnp.int32)
    trained_in, trained_out = second_round(
        sources, picks_t[:, STEPS:], pool_inputs, pool_targets, landed, hidden, scale_in, scale_out
    )
    return (trained_in, trained_out, prediction)


def solution(mesh):
    in_specs = (
        P("sub", None),
        P("sub", None),
        P(None, "sub"),
        P(None, "sub"),
        P(None, "sub"),
        P("sub", None),
        P(),
    )
    out_specs = (P(None, "sub"), P(None, "sub"), P("sub", None))
    return jax.shard_map(
        per_device, mesh=mesh, in_specs=in_specs, out_specs=out_specs, check_vma=False
    )
```

```python
import math

import jax
import jax.numpy as jnp
from jax import lax
from jax.experimental import pallas as pl
from jax.experimental.pallas import tpu as pltpu
from jax.sharding import PartitionSpec as P

D = 4096
GROUP = 8
STEPS = 4


tanh_coef = 0.7978845608028654
cubic_coef = 0.044715
step_rate = 0.5


def gelu_value(inputs):
    inner_term = tanh_coef * (inputs + cubic_coef * inputs * inputs * inputs)
    return 0.5 * inputs * (1.0 + jnp.tanh(inner_term))


def gelu_parts(inputs):
    tanh_part = jnp.tanh(tanh_coef * (inputs + cubic_coef * inputs * inputs * inputs))
    values = 0.5 * inputs * (1.0 + tanh_part)
    slopes = 0.5 * (1.0 + tanh_part) + 0.5 * inputs * (1.0 - tanh_part * tanh_part) * tanh_coef * (
        1.0 + 3.0 * cubic_coef * inputs * inputs
    )
    return (values, slopes)


NT = (((1,), (1,)), ((), ()))


def train_steps(scale_in, scale_out, picks_ref, pin_ref, ptg_ref, wi_ref, wo_ref, rows_ref):
    batch = picks_ref.shape[0]
    pool = pin_ref.shape[0]
    turns = picks_ref.shape[1]

    def one_turn(turn, carry):
        lanes = lax.broadcasted_iota(jnp.int32, (batch, turns), 1)
        picked = jnp.sum(jnp.where(lanes == turn, picks_ref[...], 0), axis=1, keepdims=True)
        onehot = (picked == lax.broadcasted_iota(jnp.int32, (batch, pool), 1)).astype(jnp.bfloat16)
        rows = jnp.dot(onehot, pin_ref[...], preferred_element_type=jnp.float32).astype(jnp.bfloat16)
        rows_ref[...] = rows
        in_half = wi_ref[...].astype(jnp.bfloat16)
        before = lax.dot_general(rows, in_half, NT, preferred_element_type=jnp.float32) * scale_in
        values, slopes = gelu_parts(before)
        activity = values.astype(jnp.bfloat16)
        activity_t = values.T.astype(jnp.bfloat16)
        goals = jnp.dot(onehot, ptg_ref[...], preferred_element_type=jnp.float32)
        out_half = wo_ref[...].astype(jnp.bfloat16)
        branch = jnp.dot(activity, out_half, preferred_element_type=jnp.float32) * scale_out
        errors = (branch - goals).astype(jnp.bfloat16)
        back = lax.dot_general(errors, out_half, NT, preferred_element_type=jnp.float32)
        grad_out = jnp.dot(activity_t, errors, preferred_element_type=jnp.float32) * scale_out
        wo_ref[...] = wo_ref[...] - step_rate * grad_out
        backward = back * scale_out * slopes
        backward_t = backward.astype(jnp.bfloat16).astype(jnp.float32).T.astype(jnp.bfloat16)
        grad_in = jnp.dot(backward_t, rows_ref[...], preferred_element_type=jnp.float32) * scale_in
        wi_ref[...] = wi_ref[...] - step_rate * grad_in
        return carry

    lax.fori_loop(0, turns, one_turn, 0)


def first_body(scale_in, scale_out, picks_ref, pin_ref, ptg_ref, wi0_ref, wo0_ref,
               inh_ref, outh_ref, wi_ref, wo_ref, rows_ref):
    wi_ref[...] = wi0_ref[...].T
    wo_ref[...] = wo0_ref[...].T
    train_steps(scale_in, scale_out, picks_ref, pin_ref, ptg_ref, wi_ref, wo_ref, rows_ref)
    inh_ref[...] = wi_ref[...].astype(jnp.bfloat16)
    outh_ref[...] = wo_ref[...].astype(jnp.bfloat16)


def second_body(scale_in, scale_out, src_ref, picks_ref, pin_ref, ptg_ref, land_ref,
                ti_ref, to_ref, wi_ref, wo_ref, rows_ref, stage_ref, sems):
    groups = stage_ref.shape[0]

    def fetch(g, carry):
        pltpu.make_async_copy(land_ref.at[src_ref[g]], stage_ref.at[g], sems.at[g]).start()
        return carry

    lax.fori_loop(0, groups, fetch, 0)

    def unpack(g, carry):
        pltpu.make_async_copy(land_ref.at[src_ref[g]], stage_ref.at[g], sems.at[g]).wait()
        block = stage_ref[g].astype(jnp.float32)
        part = pl.ds(pl.multiple_of(g * GROUP, GROUP), GROUP)
        wi_ref[part, :] = block[:GROUP]
        wo_ref[part, :] = block[GROUP:]
        return carry

    lax.fori_loop(0, groups, unpack, 0)
    train_steps(scale_in, scale_out, picks_ref, pin_ref, ptg_ref, wi_ref, wo_ref, rows_ref)
    ti_ref[...] = wi_ref[...].T
    to_ref[...] = wo_ref[...].T


def round_cost(hidden, width, batch, turns, pool):
    flops = turns * 2 * (2 * batch * pool * width + 5 * batch * hidden * width)
    return pl.CostEstimate(
        flops=flops,
        transcendentals=turns * batch * hidden,
        bytes_accessed=4 * hidden * width * 4 + 2 * pool * width * 2,
    )


VMEM_LIMIT = 63 * 1024 * 1024


def first_round(picks_t, pool_inputs, pool_targets, weight_in, weight_out, scale_in, scale_out):
    width, hidden = weight_in.shape
    batch, turns = picks_t.shape
    pool = pool_inputs.shape[0]
    vmem = pl.BlockSpec(memory_space=pltpu.VMEM)
    return pl.pallas_call(
        lambda *refs: first_body(scale_in, scale_out, *refs),
        out_shape=(
            jax.ShapeDtypeStruct((hidden, width), jnp.bfloat16),
            jax.ShapeDtypeStruct((hidden, width), jnp.bfloat16),
        ),
        in_specs=[vmem] * 5,
        out_specs=(vmem, vmem),
        scratch_shapes=[
            pltpu.VMEM((hidden, width), jnp.float32),
            pltpu.VMEM((hidden, width), jnp.float32),
            pltpu.VMEM((batch, width), jnp.bfloat16),
        ],
        compiler_params=pltpu.CompilerParams(vmem_limit_bytes=VMEM_LIMIT),
        cost_estimate=round_cost(hidden, width, batch, turns, pool),
        name="first_round",
    )(picks_t, pool_inputs, pool_targets, weight_in, weight_out)


def second_round(sources, picks_t, pool_inputs, pool_targets, landed, hidden, scale_in, scale_out):
    _, _, width = landed.shape
    batch, turns = picks_t.shape
    pool = pool_inputs.shape[0]
    groups = hidden // GROUP
    vmem = pl.BlockSpec(memory_space=pltpu.VMEM)
    return pl.pallas_call(
        lambda *refs: second_body(scale_in, scale_out, *refs),
        out_shape=(
            jax.ShapeDtypeStruct((width, hidden), jnp.float32),
            jax.ShapeDtypeStruct((width, hidden), jnp.float32),
        ),
        in_specs=[pl.BlockSpec(memory_space=pltpu.SMEM), vmem, vmem, vmem,
                  pl.BlockSpec(memory_space=pl.ANY)],
        out_specs=(vmem, vmem),
        scratch_shapes=[
            pltpu.VMEM((hidden, width), jnp.float32),
            pltpu.VMEM((hidden, width), jnp.float32),
            pltpu.VMEM((batch, width), jnp.bfloat16),
            pltpu.VMEM((groups, 2 * GROUP, width), jnp.bfloat16),
            pltpu.SemaphoreType.DMA((groups,)),
        ],
        compiler_params=pltpu.CompilerParams(vmem_limit_bytes=VMEM_LIMIT),
        cost_estimate=round_cost(hidden, width, batch, turns, pool),
        name="second_round",
    )(sources, picks_t, pool_inputs, pool_targets, landed)


def per_device(pool_inputs, pool_targets, row_picks, weight_in, weight_out, eval_inputs, handover):
    owners = lax.axis_size("sub")
    my_index = lax.axis_index("sub")
    hidden = weight_in.shape[1]
    group_count = hidden // GROUP
    scale_in = 1.0 / math.sqrt(D)
    scale_out = 1.0 / math.sqrt(hidden * owners)
    eval_all = lax.all_to_all(
        jnp.broadcast_to(eval_inputs[None], (owners,) + eval_inputs.shape), "sub", 0, 0, tiled=True
    ).reshape(owners * eval_inputs.shape[0], eval_inputs.shape[1])
    picks_t = row_picks.T
    in_half, out_half = first_round(
        picks_t[:, :STEPS], pool_inputs, pool_targets, weight_in, weight_out, scale_in, scale_out
    )
    pieces = owners
    piece = 2 * GROUP * D // pieces
    splits = pieces // (2 * GROUP)
    stacked = jnp.concatenate(
        [in_half.reshape(group_count, GROUP, D), out_half.reshape(group_count, GROUP, D)], axis=1
    )
    spread = (
        stacked.reshape(group_count, 2 * GROUP, splits, piece)
        .transpose(1, 2, 0, 3)
        .reshape(pieces, group_count, piece)
    )
    held = lax.all_to_all(spread, "sub", 0, 0, tiled=True).reshape(owners * group_count, piece)
    total_groups = owners * group_count
    inverse = (
        jnp.zeros((total_groups,), jnp.int32)
        .at[handover]
        .set(jnp.arange(total_groups, dtype=jnp.int32))
    )
    forward = jnp.take(held, inverse, axis=0, mode="clip").reshape(
        owners, group_count, piece
    )
    arrived = lax.all_to_all(forward, "sub", 0, 0, tiled=True)
    landed = (
        arrived.reshape(2 * GROUP, splits, group_count, piece)
        .transpose(2, 0, 1, 3)
        .reshape(group_count, 2 * GROUP, D)
    )
    eval_act = gelu_value(
        lax.dot_general(eval_all, in_half, NT, preferred_element_type=jnp.float32) * scale_in
    ).astype(jnp.bfloat16)
    partial = jnp.dot(eval_act, out_half, preferred_element_type=jnp.float32) * scale_out
    rows_each = partial.shape[0] // owners
    parity = my_index % 2
    split = partial.reshape(owners // 2, 2, rows_each, partial.shape[1])
    mine = jnp.where(parity == 0, split[:, 0], split[:, 1])
    other = jnp.where(parity == 0, split[:, 1], split[:, 0])
    mine, other, landed = lax.optimization_barrier((mine, other, landed))
    pairs = [(k, k ^ 1) for k in range(owners)]
    summed = mine + lax.ppermute(other, "sub", perm=pairs)
    same_parity = [list(range(0, owners, 2)), list(range(1, owners, 2))]
    gathered = lax.all_to_all(summed, "sub", 0, 0, tiled=True, axis_index_groups=same_parity)
    prediction = jnp.sum(gathered, axis=0)

    sources = jnp.arange(group_count, dtype=jnp.int32)
    trained_in, trained_out = second_round(
        sources, picks_t[:, STEPS:], pool_inputs, pool_targets, landed, hidden, scale_in, scale_out
    )
    return (trained_in, trained_out, prediction)


def solution(mesh):
    in_specs = (
        P("sub", None),
        P("sub", None),
        P(None, "sub"),
        P(None, "sub"),
        P(None, "sub"),
        P("sub", None),
        P(),
    )
    out_specs = (P(None, "sub"), P(None, "sub"), P("sub", None))
    return jax.shard_map(
        per_device, mesh=mesh, in_specs=in_specs, out_specs=out_specs, check_vma=False
    )
```

```python
import math

import jax
import jax.numpy as jnp
from jax import lax
from jax.experimental import pallas as pl
from jax.experimental.pallas import tpu as pltpu
from jax.sharding import PartitionSpec as P

D = 4096
GROUP = 8
STEPS = 4


tanh_coef = 0.7978845608028654
cubic_coef = 0.044715
step_rate = 0.5


def gelu_value(inputs):
    inner_term = tanh_coef * (inputs + cubic_coef * inputs * inputs * inputs)
    return 0.5 * inputs * (1.0 + jnp.tanh(inner_term))


def gelu_parts(inputs):
    tanh_part = jnp.tanh(tanh_coef * (inputs + cubic_coef * inputs * inputs * inputs))
    values = 0.5 * inputs * (1.0 + tanh_part)
    slopes = 0.5 * (1.0 + tanh_part) + 0.5 * inputs * (1.0 - tanh_part * tanh_part) * tanh_coef * (
        1.0 + 3.0 * cubic_coef * inputs * inputs
    )
    return (values, slopes)


NT = (((1,), (1,)), ((), ()))


def train_steps(scale_in, scale_out, picks_ref, pin_ref, ptg_ref, wi_ref, wo_ref, rows_ref):
    batch = picks_ref.shape[0]
    pool = pin_ref.shape[0]
    turns = picks_ref.shape[1]

    def one_turn(turn, carry):
        lanes = lax.broadcasted_iota(jnp.int32, (batch, turns), 1)
        picked = jnp.sum(jnp.where(lanes == turn, picks_ref[...], 0), axis=1, keepdims=True)
        onehot = (picked == lax.broadcasted_iota(jnp.int32, (batch, pool), 1)).astype(jnp.bfloat16)
        rows = jnp.dot(onehot, pin_ref[...], preferred_element_type=jnp.float32).astype(jnp.bfloat16)
        rows_ref[...] = rows
        in_half = wi_ref[...].astype(jnp.bfloat16)
        before = lax.dot_general(rows, in_half, NT, preferred_element_type=jnp.float32) * scale_in
        values, slopes = gelu_parts(before)
        activity = values.astype(jnp.bfloat16)
        activity_t = values.T.astype(jnp.bfloat16)
        goals = jnp.dot(onehot, ptg_ref[...], preferred_element_type=jnp.float32)
        out_half = wo_ref[...].astype(jnp.bfloat16)
        branch = jnp.dot(activity, out_half, preferred_element_type=jnp.float32) * scale_out
        errors = (branch - goals).astype(jnp.bfloat16)
        back = lax.dot_general(errors, out_half, NT, preferred_element_type=jnp.float32)
        grad_out = jnp.dot(activity_t, errors, preferred_element_type=jnp.float32) * scale_out
        wo_ref[...] = wo_ref[...] - step_rate * grad_out
        backward = back * scale_out * slopes
        backward_t = backward.astype(jnp.bfloat16).astype(jnp.float32).T.astype(jnp.bfloat16)
        grad_in = jnp.dot(backward_t, rows_ref[...], preferred_element_type=jnp.float32) * scale_in
        wi_ref[...] = wi_ref[...] - step_rate * grad_in
        return carry

    lax.fori_loop(0, turns, one_turn, 0)


def first_body(scale_in, scale_out, picks_ref, pin_ref, ptg_ref, wi0_ref, wo0_ref,
               inh_ref, outh_ref, wi_ref, wo_ref, rows_ref):
    wi_ref[...] = wi0_ref[...].T
    wo_ref[...] = wo0_ref[...].T
    train_steps(scale_in, scale_out, picks_ref, pin_ref, ptg_ref, wi_ref, wo_ref, rows_ref)
    inh_ref[...] = wi_ref[...].astype(jnp.bfloat16)
    outh_ref[...] = wo_ref[...].astype(jnp.bfloat16)


def second_body(scale_in, scale_out, src_ref, picks_ref, pin_ref, ptg_ref, land_ref,
                ti_ref, to_ref, wi_ref, wo_ref, rows_ref, stage_ref, sems):
    groups = stage_ref.shape[0]

    def fetch(g, carry):
        pltpu.make_async_copy(land_ref.at[src_ref[g]], stage_ref.at[g], sems.at[g]).start()
        return carry

    lax.fori_loop(0, groups, fetch, 0)

    def unpack(g, carry):
        pltpu.make_async_copy(land_ref.at[src_ref[g]], stage_ref.at[g], sems.at[g]).wait()
        block = stage_ref[g].astype(jnp.float32)
        part = pl.ds(pl.multiple_of(g * GROUP, GROUP), GROUP)
        wi_ref[part, :] = block[:GROUP]
        wo_ref[part, :] = block[GROUP:]
        return carry

    lax.fori_loop(0, groups, unpack, 0)
    train_steps(scale_in, scale_out, picks_ref, pin_ref, ptg_ref, wi_ref, wo_ref, rows_ref)
    ti_ref[...] = wi_ref[...].T
    to_ref[...] = wo_ref[...].T


def round_cost(hidden, width, batch, turns, pool):
    flops = turns * 2 * (2 * batch * pool * width + 5 * batch * hidden * width)
    return pl.CostEstimate(
        flops=flops,
        transcendentals=turns * batch * hidden,
        bytes_accessed=4 * hidden * width * 4 + 2 * pool * width * 2,
    )


VMEM_LIMIT = 63 * 1024 * 1024


def first_round(picks_t, pool_inputs, pool_targets, weight_in, weight_out, scale_in, scale_out):
    width, hidden = weight_in.shape
    batch, turns = picks_t.shape
    pool = pool_inputs.shape[0]
    vmem = pl.BlockSpec(memory_space=pltpu.VMEM)
    return pl.pallas_call(
        lambda *refs: first_body(scale_in, scale_out, *refs),
        out_shape=(
            jax.ShapeDtypeStruct((hidden, width), jnp.bfloat16),
            jax.ShapeDtypeStruct((hidden, width), jnp.bfloat16),
        ),
        in_specs=[vmem] * 5,
        out_specs=(vmem, vmem),
        scratch_shapes=[
            pltpu.VMEM((hidden, width), jnp.float32),
            pltpu.VMEM((hidden, width), jnp.float32),
            pltpu.VMEM((batch, width), jnp.bfloat16),
        ],
        compiler_params=pltpu.CompilerParams(vmem_limit_bytes=VMEM_LIMIT),
        cost_estimate=round_cost(hidden, width, batch, turns, pool),
        name="first_round",
    )(picks_t, pool_inputs, pool_targets, weight_in, weight_out)


def second_round(sources, picks_t, pool_inputs, pool_targets, landed, hidden, scale_in, scale_out):
    _, _, width = landed.shape
    batch, turns = picks_t.shape
    pool = pool_inputs.shape[0]
    groups = hidden // GROUP
    vmem = pl.BlockSpec(memory_space=pltpu.VMEM)
    return pl.pallas_call(
        lambda *refs: second_body(scale_in, scale_out, *refs),
        out_shape=(
            jax.ShapeDtypeStruct((width, hidden), jnp.float32),
            jax.ShapeDtypeStruct((width, hidden), jnp.float32),
        ),
        in_specs=[pl.BlockSpec(memory_space=pltpu.SMEM), vmem, vmem, vmem,
                  pl.BlockSpec(memory_space=pl.ANY)],
        out_specs=(vmem, vmem),
        scratch_shapes=[
            pltpu.VMEM((hidden, width), jnp.float32),
            pltpu.VMEM((hidden, width), jnp.float32),
            pltpu.VMEM((batch, width), jnp.bfloat16),
            pltpu.VMEM((groups, 2 * GROUP, width), jnp.bfloat16),
            pltpu.SemaphoreType.DMA((groups,)),
        ],
        compiler_params=pltpu.CompilerParams(vmem_limit_bytes=VMEM_LIMIT),
        cost_estimate=round_cost(hidden, width, batch, turns, pool),
        name="second_round",
    )(sources, picks_t, pool_inputs, pool_targets, landed)


def per_device(pool_inputs, pool_targets, row_picks, weight_in, weight_out, eval_inputs, handover):
    owners = lax.axis_size("sub")
    my_index = lax.axis_index("sub")
    hidden = weight_in.shape[1]
    group_count = hidden // GROUP
    scale_in = 1.0 / math.sqrt(D)
    scale_out = 1.0 / math.sqrt(hidden * owners)
    eval_all = lax.all_to_all(
        jnp.broadcast_to(eval_inputs[None], (owners,) + eval_inputs.shape), "sub", 0, 0, tiled=True
    ).reshape(owners * eval_inputs.shape[0], eval_inputs.shape[1])
    picks_t = row_picks.T
    in_half, out_half = first_round(
        picks_t[:, :STEPS], pool_inputs, pool_targets, weight_in, weight_out, scale_in, scale_out
    )
    pieces = owners
    piece = 2 * GROUP * D // pieces
    splits = pieces // (2 * GROUP)
    stacked = jnp.concatenate(
        [in_half.reshape(group_count, GROUP, D), out_half.reshape(group_count, GROUP, D)], axis=1
    )
    spread = (
        stacked.reshape(group_count, 2 * GROUP, splits, piece)
        .transpose(1, 2, 0, 3)
        .reshape(pieces, group_count, piece)
    )
    held = lax.all_to_all(spread, "sub", 0, 0, tiled=True).reshape(owners * group_count, piece)
    total_groups = owners * group_count
    inverse = (
        jnp.zeros((total_groups,), jnp.int32)
        .at[handover]
        .set(jnp.arange(total_groups, dtype=jnp.int32))
    )
    forward = jnp.take(held, inverse, axis=0, mode="clip").reshape(
        owners, group_count, piece
    )
    arrived = lax.all_to_all(forward, "sub", 0, 0, tiled=True)
    landed = (
        arrived.reshape(2 * GROUP, splits, group_count, piece)
        .transpose(2, 0, 1, 3)
        .reshape(group_count, 2 * GROUP, D)
    )
    eval_act = gelu_value(
        lax.dot_general(eval_all, in_half, NT, preferred_element_type=jnp.float32) * scale_in
    ).astype(jnp.bfloat16)
    partial = jnp.dot(eval_act, out_half, preferred_element_type=jnp.float32) * scale_out
    rows_each = partial.shape[0] // owners
    parity = my_index % 2
    split = partial.reshape(owners // 2, 2, rows_each, partial.shape[1])
    mine = jnp.where(parity == 0, split[:, 0], split[:, 1])
    other = jnp.where(parity == 0, split[:, 1], split[:, 0])
    pairs = [(k, k ^ 1) for k in range(owners)]
    summed = mine + lax.ppermute(other, "sub", perm=pairs)
    summed, landed = lax.optimization_barrier((summed, landed))
    same_parity = [list(range(0, owners, 2)), list(range(1, owners, 2))]
    gathered = lax.all_to_all(summed, "sub", 0, 0, tiled=True, axis_index_groups=same_parity)
    prediction = jnp.sum(gathered, axis=0)

    sources = jnp.arange(group_count, dtype=jnp.int32)
    trained_in, trained_out = second_round(
        sources, picks_t[:, STEPS:], pool_inputs, pool_targets, landed, hidden, scale_in, scale_out
    )
    return (trained_in, trained_out, prediction)


def solution(mesh):
    in_specs = (
        P("sub", None),
        P("sub", None),
        P(None, "sub"),
        P(None, "sub"),
        P(None, "sub"),
        P("sub", None),
        P(),
    )
    out_specs = (P(None, "sub"), P(None, "sub"), P("sub", None))
    return jax.shard_map(
        per_device, mesh=mesh, in_specs=in_specs, out_specs=out_specs, check_vma=False
    )
```

```python
import math

import jax
import jax.numpy as jnp
from jax import lax
from jax.experimental import pallas as pl
from jax.experimental.pallas import tpu as pltpu
from jax.sharding import PartitionSpec as P

D = 4096
GROUP = 8
STEPS = 4


tanh_coef = 0.7978845608028654
cubic_coef = 0.044715
step_rate = 0.5


def gelu_value(inputs):
    inner_term = tanh_coef * (inputs + cubic_coef * inputs * inputs * inputs)
    return 0.5 * inputs * (1.0 + jnp.tanh(inner_term))


def gelu_parts(inputs):
    tanh_part = jnp.tanh(tanh_coef * (inputs + cubic_coef * inputs * inputs * inputs))
    values = 0.5 * inputs * (1.0 + tanh_part)
    slopes = 0.5 * (1.0 + tanh_part) + 0.5 * inputs * (1.0 - tanh_part * tanh_part) * tanh_coef * (
        1.0 + 3.0 * cubic_coef * inputs * inputs
    )
    return (values, slopes)


NT = (((1,), (1,)), ((), ()))


def train_steps(scale_in, scale_out, picks_ref, pin_ref, ptg_ref, wi_ref, wo_ref, rows_ref):
    batch = picks_ref.shape[0]
    pool = pin_ref.shape[0]
    turns = picks_ref.shape[1]

    def one_turn(turn, carry):
        lanes = lax.broadcasted_iota(jnp.int32, (batch, turns), 1)
        picked = jnp.sum(jnp.where(lanes == turn, picks_ref[...], 0), axis=1, keepdims=True)
        onehot = (picked == lax.broadcasted_iota(jnp.int32, (batch, pool), 1)).astype(jnp.bfloat16)
        rows = jnp.dot(onehot, pin_ref[...], preferred_element_type=jnp.float32).astype(jnp.bfloat16)
        rows_ref[...] = rows
        in_half = wi_ref[...].astype(jnp.bfloat16)
        before = lax.dot_general(rows, in_half, NT, preferred_element_type=jnp.float32) * scale_in
        values, slopes = gelu_parts(before)
        activity = values.astype(jnp.bfloat16)
        activity_t = values.T.astype(jnp.bfloat16)
        goals = jnp.dot(onehot, ptg_ref[...], preferred_element_type=jnp.float32)
        out_half = wo_ref[...].astype(jnp.bfloat16)
        branch = jnp.dot(activity, out_half, preferred_element_type=jnp.float32) * scale_out
        errors = (branch - goals).astype(jnp.bfloat16)
        back = lax.dot_general(errors, out_half, NT, preferred_element_type=jnp.float32)
        grad_out = jnp.dot(activity_t, errors, preferred_element_type=jnp.float32) * scale_out
        wo_ref[...] = wo_ref[...] - step_rate * grad_out
        backward = back * scale_out * slopes
        backward_t = backward.astype(jnp.bfloat16).astype(jnp.float32).T.astype(jnp.bfloat16)
        grad_in = jnp.dot(backward_t, rows_ref[...], preferred_element_type=jnp.float32) * scale_in
        wi_ref[...] = wi_ref[...] - step_rate * grad_in
        return carry

    lax.fori_loop(0, turns, one_turn, 0)


def first_body(scale_in, scale_out, picks_ref, pin_ref, ptg_ref, wi0_ref, wo0_ref,
               inh_ref, outh_ref, wi_ref, wo_ref, rows_ref):
    wi_ref[...] = wi0_ref[...].T
    wo_ref[...] = wo0_ref[...].T
    train_steps(scale_in, scale_out, picks_ref, pin_ref, ptg_ref, wi_ref, wo_ref, rows_ref)
    inh_ref[...] = wi_ref[...].astype(jnp.bfloat16)
    outh_ref[...] = wo_ref[...].astype(jnp.bfloat16)


def second_body(scale_in, scale_out, src_ref, picks_ref, pin_ref, ptg_ref, land_ref,
                ti_ref, to_ref, wi_ref, wo_ref, rows_ref, stage_ref, sems):
    groups = stage_ref.shape[0]

    def fetch(g, carry):
        pltpu.make_async_copy(land_ref.at[src_ref[g]], stage_ref.at[g], sems.at[g]).start()
        return carry

    lax.fori_loop(0, groups, fetch, 0)

    def unpack(g, carry):
        pltpu.make_async_copy(land_ref.at[src_ref[g]], stage_ref.at[g], sems.at[g]).wait()
        block = stage_ref[g].astype(jnp.float32)
        part = pl.ds(pl.multiple_of(g * GROUP, GROUP), GROUP)
        wi_ref[part, :] = block[:GROUP]
        wo_ref[part, :] = block[GROUP:]
        return carry

    lax.fori_loop(0, groups, unpack, 0)
    train_steps(scale_in, scale_out, picks_ref, pin_ref, ptg_ref, wi_ref, wo_ref, rows_ref)
    ti_ref[...] = wi_ref[...].T
    to_ref[...] = wo_ref[...].T


def round_cost(hidden, width, batch, turns, pool):
    flops = turns * 2 * (2 * batch * pool * width + 5 * batch * hidden * width)
    return pl.CostEstimate(
        flops=flops,
        transcendentals=turns * batch * hidden,
        bytes_accessed=4 * hidden * width * 4 + 2 * pool * width * 2,
    )


VMEM_LIMIT = 63 * 1024 * 1024


def first_round(picks_t, pool_inputs, pool_targets, weight_in, weight_out, scale_in, scale_out):
    width, hidden = weight_in.shape
    batch, turns = picks_t.shape
    pool = pool_inputs.shape[0]
    vmem = pl.BlockSpec(memory_space=pltpu.VMEM)
    return pl.pallas_call(
        lambda *refs: first_body(scale_in, scale_out, *refs),
        out_shape=(
            jax.ShapeDtypeStruct((hidden, width), jnp.bfloat16),
            jax.ShapeDtypeStruct((hidden, width), jnp.bfloat16),
        ),
        in_specs=[vmem] * 5,
        out_specs=(vmem, vmem),
        scratch_shapes=[
            pltpu.VMEM((hidden, width), jnp.float32),
            pltpu.VMEM((hidden, width), jnp.float32),
            pltpu.VMEM((batch, width), jnp.bfloat16),
        ],
        compiler_params=pltpu.CompilerParams(vmem_limit_bytes=VMEM_LIMIT),
        cost_estimate=round_cost(hidden, width, batch, turns, pool),
        name="first_round",
    )(picks_t, pool_inputs, pool_targets, weight_in, weight_out)


def second_round(sources, picks_t, pool_inputs, pool_targets, landed, hidden, scale_in, scale_out):
    _, _, width = landed.shape
    batch, turns = picks_t.shape
    pool = pool_inputs.shape[0]
    groups = hidden // GROUP
    vmem = pl.BlockSpec(memory_space=pltpu.VMEM)
    return pl.pallas_call(
        lambda *refs: second_body(scale_in, scale_out, *refs),
        out_shape=(
            jax.ShapeDtypeStruct((width, hidden), jnp.float32),
            jax.ShapeDtypeStruct((width, hidden), jnp.float32),
        ),
        in_specs=[pl.BlockSpec(memory_space=pltpu.SMEM), vmem, vmem, vmem,
                  pl.BlockSpec(memory_space=pl.ANY)],
        out_specs=(vmem, vmem),
        scratch_shapes=[
            pltpu.VMEM((hidden, width), jnp.float32),
            pltpu.VMEM((hidden, width), jnp.float32),
            pltpu.VMEM((batch, width), jnp.bfloat16),
            pltpu.VMEM((groups, 2 * GROUP, width), jnp.bfloat16),
            pltpu.SemaphoreType.DMA((groups,)),
        ],
        compiler_params=pltpu.CompilerParams(vmem_limit_bytes=VMEM_LIMIT),
        cost_estimate=round_cost(hidden, width, batch, turns, pool),
        name="second_round",
    )(sources, picks_t, pool_inputs, pool_targets, landed)


def per_device(pool_inputs, pool_targets, row_picks, weight_in, weight_out, eval_inputs, handover):
    owners = lax.axis_size("sub")
    my_index = lax.axis_index("sub")
    hidden = weight_in.shape[1]
    group_count = hidden // GROUP
    scale_in = 1.0 / math.sqrt(D)
    scale_out = 1.0 / math.sqrt(hidden * owners)
    eval_all = lax.all_to_all(
        jnp.broadcast_to(eval_inputs[None], (owners,) + eval_inputs.shape), "sub", 0, 0, tiled=True
    ).reshape(owners * eval_inputs.shape[0], eval_inputs.shape[1])
    picks_t = row_picks.T
    in_half, out_half = first_round(
        picks_t[:, :STEPS], pool_inputs, pool_targets, weight_in, weight_out, scale_in, scale_out
    )
    pieces = owners
    piece = 2 * GROUP * D // pieces
    splits = pieces // (2 * GROUP)
    stacked = jnp.concatenate(
        [in_half.reshape(group_count, GROUP, D), out_half.reshape(group_count, GROUP, D)], axis=1
    )
    spread = (
        stacked.reshape(group_count, 2 * GROUP, splits, piece)
        .transpose(1, 2, 0, 3)
        .reshape(pieces, group_count, piece)
    )
    held = lax.all_to_all(spread, "sub", 0, 0, tiled=True).reshape(owners * group_count, piece)
    total_groups = owners * group_count
    inverse = (
        jnp.zeros((total_groups,), jnp.int32)
        .at[handover]
        .set(jnp.arange(total_groups, dtype=jnp.int32))
    )
    forward = held.at[inverse].get(mode="clip", unique_indices=True).reshape(
        owners, group_count, piece
    )
    arrived = lax.all_to_all(forward, "sub", 0, 0, tiled=True)
    landed = (
        arrived.reshape(2 * GROUP, splits, group_count, piece)
        .transpose(2, 0, 1, 3)
        .reshape(group_count, 2 * GROUP, D)
    )
    eval_act = gelu_value(
        lax.dot_general(eval_all, in_half, NT, preferred_element_type=jnp.float32) * scale_in
    ).astype(jnp.bfloat16)
    partial = jnp.dot(eval_act, out_half, preferred_element_type=jnp.float32) * scale_out
    rows_each = partial.shape[0] // owners
    parity = my_index % 2
    split = partial.reshape(owners // 2, 2, rows_each, partial.shape[1])
    mine = jnp.where(parity == 0, split[:, 0], split[:, 1])
    other = jnp.where(parity == 0, split[:, 1], split[:, 0])
    pairs = [(k, k ^ 1) for k in range(owners)]
    summed = mine + lax.ppermute(other, "sub", perm=pairs)
    summed, landed = lax.optimization_barrier((summed, landed))
    same_parity = [list(range(0, owners, 2)), list(range(1, owners, 2))]
    gathered = lax.all_to_all(summed, "sub", 0, 0, tiled=True, axis_index_groups=same_parity)
    prediction = jnp.sum(gathered, axis=0)

    sources = jnp.arange(group_count, dtype=jnp.int32)
    trained_in, trained_out = second_round(
        sources, picks_t[:, STEPS:], pool_inputs, pool_targets, landed, hidden, scale_in, scale_out
    )
    return (trained_in, trained_out, prediction)


def solution(mesh):
    in_specs = (
        P("sub", None),
        P("sub", None),
        P(None, "sub"),
        P(None, "sub"),
        P(None, "sub"),
        P("sub", None),
        P(),
    )
    out_specs = (P(None, "sub"), P(None, "sub"), P("sub", None))
    return jax.shard_map(
        per_device, mesh=mesh, in_specs=in_specs, out_specs=out_specs, check_vma=False
    )
```
